128 devices in a mesh: dp: 4 (over y), seq: 8 (over z, x_hi), tensor: 4 (over x_lo, core).
Axes of the slice: x: 4 (x_hi: 2, x_lo: 2; x = x_hi * 2 + x_lo), y: 4, z: 4, core: 2. Of those that a mesh axis runs over, the one named last changes fastest.
Arguments:
- patches: bfloat16 [16384, 1664], P(('dp', 'seq')), parts along dimension 0, may hold values from -6 to 6
- image_sizes: int32 [76, 2], P('dp'), parts along dimension 0, may hold values from 0 to 32, as said below
- seg_ids: int32 [16384], P('dp'), parts along dimension 0, may hold values from 0 to 19, as said below
- pad_mask: int32 [16384], P('dp'), parts along dimension 0, may hold values from 0 to 1, as said below
- ln1_gain: float32 [1664], replicated, may hold values from 0.1 to 1.9
- qkv_weight: bfloat16 [1664, 3, 1664], P(None, None, 'tensor')
- out_weight: bfloat16 [1664, 1664], P('tensor'), may hold values from -0.15625 to 0.15625
- ln2_gain: float32 [1664], replicated, may hold values from 0.1 to 1.9
- fc1_weight: bfloat16 [1664, 8192], P(None, 'tensor'), may hold values from -0.15625 to 0.15625
- fc2_weight: bfloat16 [8192, 1664], P('tensor'), may hold values from -0.0625 to 0.0625
- proj_weight: bfloat16 [6656, 4096], P('tensor', 'seq'), may hold values from -0.078125 to 0.078125
- owners: int32 [4096, 1], P('dp'), parts along dimension 0, may hold values from 0 to 7; in each aligned block of 256 rows (0 to 255, 256 to 511, ...) at most 64 rows name the same one
Outputs:
- delivered: bfloat16 [32, 4, 64, 4096], P(('dp', 'seq'), 'tensor'), parts along dimension 0
- image_rms: float32 [76], P('dp'), parts along dimension 0
- image_peak: float32 [76], P('dp'), parts along dimension 0
The draws below stay inside these ranges and needn't reach their ends.
There are 4 independent parts, one for each index of `dp`. The reference program is written for one: setup_inputs(seed, part) draws one part's arguments, and reference() takes and returns one part's arrays. A program takes and returns all parts, laid end to end along the dimension named above; an argument that names none is the same for every part. Nothing has to cross between parts.
Inputs may be any that keep to these rules, and one draw needn't show every extreme that they name: `image_sizes`: sides are even; slots are packed in slot order from token 0 without gaps; the padding after the last image is shorter than 512 tokens; some slots are 0 x 0. `seg_ids`: consistent with image_sizes: tokens of slot i in order, then 19 for the padding. `pad_mask`: 1 exactly on tokens of the images. `owners`: in each aligned block of 256 merged rows no owner is named by more than 64 rows, and one is named by exactly 64.
All inputs are finite; a program needn't handle non-finite values.
Results may differ from the reference program's by a relative error of at most 0.017.
Values may be sent and summed in bfloat16 or wider, within the bound.
No kernel may reach another device: no remote copies, remote signals or barrier semaphores. Data moves between devices by JAX's collectives and lax.ppermute only.
A program may use at most 128 MiB of HBM per device.

```python
import math
import jax
import jax.numpy as jnp
import numpy as np
from jax import lax

D = 1664
NH = 16
HD = 104
FF = 8192
PROJ = 4096
SIDE = 32
TOK_DEV = 512
TOKENS = 4096
NIMG = 19
MROWS = 1024
QROWS = 256
CAP = 64
N_SEQ = 8
N_TENSOR = 4


def pack_layout(key):
    inner = jax.random.fold_in(key, 11)
    first_key, second_key, third_key = jax.random.split(inner, 3)
    count = NIMG - 3
    heights = 2 * jax.random.randint(first_key, (count,), SIDE // 4, SIDE // 2 + 1)
    widths = 2 * jax.random.randint(second_key, (count,), SIDE // 4, SIDE // 2 + 1)
    last_height = 2 * (min(SIDE * SIDE, TOKENS - TOK_DEV) // (2 * SIDE))
    last_area = last_height * SIDE
    padding = 4 * jax.random.randint(third_key, (), 1, TOK_DEV // 4)
    region = TOKENS - last_area - padding
    kept = jnp.cumsum(heights * widths) <= region
    heights = jnp.where(kept, heights, 0)
    widths = jnp.where(kept, widths, 0)
    remainder = region - jnp.sum(heights * widths)
    quads = remainder // 4
    half_side = SIDE // 2
    fill_height = 2 * (quads // half_side)
    fill_width = jnp.where(fill_height > 0, SIDE, 0)
    small_width = 2 * (quads % half_side)
    small_height = jnp.where(small_width > 0, 2, 0)
    heights = jnp.concatenate([heights, jnp.stack([fill_height, small_height, jnp.array(last_height, heights.dtype)])])
    widths = jnp.concatenate([widths, jnp.stack([fill_width, small_width, jnp.array(SIDE, widths.dtype)])])
    ends = jnp.cumsum(heights * widths)
    filled = ends[NIMG - 1]
    index = jnp.arange(TOKENS)
    segment = jnp.sum((index[:, None] >= ends[None, :]).astype(jnp.int32), axis=1)
    segment = jnp.where(index >= filled, NIMG, segment)
    inside = (index < filled).astype(jnp.int32)
    sizes = jnp.stack([heights, widths], axis=1)
    return (sizes.astype(jnp.int32), segment.astype(jnp.int32), inside)


def draw_image_sizes(key, part):
    return pack_layout(key)[0]


def draw_seg_ids(key, part):
    return pack_layout(key)[1]


def draw_pad_mask(key, part):
    return pack_layout(key)[2]


def draw_qkv_weight(key, part):
    values = jax.random.normal(jax.random.fold_in(key, 23), (D, 3, D), jnp.float32) * D ** (-0.5)
    return values.astype(jnp.bfloat16)


def shard_levels(key, shape, cuts, low, largest):
    level, own = 1.0, jax.random.fold_in(key, 6)
    for position, blocks in cuts:
        steps = jnp.exp(jax.random.uniform(jax.random.fold_in(own, position), (blocks,), jnp.float32, low / len(cuts), largest / len(cuts)))
        level = level * jnp.repeat(steps, shape[position] // blocks).reshape([-1 if axis == position else 1 for axis in range(len(shape))])
    return level


def deal_out(own_key, own, number, rows, number_of, top, bound, skew):
    ranking = jax.random.permutation(own_key, number_of)
    crowded, ordinary = portions_of(number_of, rows * top, bound, skew, True), portions_of(number_of, rows * top, bound, skew, False)
    places = jnp.arange(number_of)

    def named(lengths, rotation):
        used = int((lengths > 0).sum())
        fixed = max(1, used // 4)
        shifted = fixed + (places - fixed + rotation * (used - fixed)) % max(1, number_of - fixed)
        return jnp.zeros((number_of,), jnp.int32).at[ranking[jnp.where(places < fixed, places, shifted)]].set(jnp.asarray(lengths, jnp.int32))

    lengths = jnp.where(number % 4 == 0, named(crowded, number // 4), named(ordinary, number - number // 4 - 1))
    mixed = jax.random.permutation(jax.random.fold_in(own, 3), number_of)
    source_of, taker = mixed[0:number_of // 2 * 2:2], mixed[1:number_of // 2 * 2:2]
    room = jnp.minimum(lengths[source_of] - 1, bound - lengths[taker]) // 2
    room = jnp.where((source_of == ranking[0]) | (taker == ranking[0]) | (lengths[taker] == 0), 0, jnp.maximum(room, 0))
    shifted = jax.random.randint(jax.random.fold_in(own, 4), (number_of // 2,), 0, 1 << 20) % (room + 1)
    lengths = lengths.at[source_of].add(-shifted).at[taker].add(shifted)
    members = jnp.searchsorted(jnp.cumsum(lengths), jnp.arange(rows * top), side="right").astype(jnp.int32)
    listing = members.reshape(top, rows).T
    listing = listing[jax.random.permutation(jax.random.fold_in(own, 1), rows)]
    rotation = jax.random.randint(jax.random.fold_in(own, 2), (rows, 1), 0, top)
    return jnp.take_along_axis(listing, (jnp.arange(top)[None, :] + rotation) % top, axis=1)


def portions_of(amount, total, bound, lean, full):
    loads = [(1 << 20) // math.isqrt(grade ** lean) + 1 for grade in range(1, amount + 1)]
    largest = bound if full else min(bound, max(-(-total // amount), total * loads[0] // sum(loads)))
    least = 1 if total - largest >= amount - 1 else 0
    given, surplus = [largest] + [least] * (amount - 1), total - largest - least * (amount - 1)
    while surplus > 0:
        free = [i for i in range(1, amount) if given[i] < largest] or [i for i in range(1, amount) if given[i] < bound]
        whole, budget = sum([loads[i] for i in free]), surplus
        for i in free:
            addition = min(bound - given[i], max(1, budget * loads[i] // whole), surplus)
            given[i] = given[i] + addition
            surplus = surplus - addition
    return np.array(given)


def gaussian(rng, dims, scale, limit, shards=(), held_as=jnp.bfloat16):
    values = jax.random.normal(rng, dims, jnp.float32) * scale
    if len(shards) > 0:
        values = shard_levels(rng, dims, shards, -0.22, 0.18) * values
    return jnp.clip(values, min=-limit, max=limit).astype(held_as)


def setup_inputs(seed: int = 0, part: int = 0) -> dict:
    arg_keys = jax.random.split(jax.random.key(seed), 13)
    part_splits = jax.random.split(jax.random.fold_in(arg_keys[12], part), 13)
    patches = gaussian(part_splits[0], (TOKENS, D), 1.0, 6.0, ((0, 8),))
    image_sizes = draw_image_sizes(jax.random.fold_in(jax.random.fold_in(arg_keys[12], part), 71), part)
    seg_ids = draw_seg_ids(jax.random.fold_in(jax.random.fold_in(arg_keys[12], part), 71), part)
    pad_mask = draw_pad_mask(jax.random.fold_in(jax.random.fold_in(arg_keys[12], part), 71), part)
    ln1_gain = jnp.clip(1.0 + 0.18 * jax.random.normal(arg_keys[4], (D,), jnp.float32), 0.1, 1.9)
    qkv_weight = draw_qkv_weight(jax.random.fold_in(arg_keys[12], 71), part)
    out_weight = gaussian(arg_keys[6], (D, D), D ** -0.5, 0.15625, ((0, 4),))
    ln2_gain = jnp.clip(1.0 + 0.18 * jax.random.normal(arg_keys[7], (D,), jnp.float32), 0.1, 1.9)
    fc1_weight = gaussian(arg_keys[8], (D, FF), D ** -0.5, 0.15625, ((1, 4),))
    fc2_weight = gaussian(arg_keys[9], (FF, D), FF ** -0.5, 0.0625, ((0, 4),))
    proj_weight = gaussian(arg_keys[10], (4 * D, PROJ), (4 * D) ** -0.5, 0.078125, ((0, 4), (1, 8)))
    owners_keys = jax.random.split(jax.random.fold_in(part_splits[11], 1), MROWS // QROWS)
    owners_turns = jax.random.permutation(jax.random.fold_in(part_splits[11], 3), MROWS // QROWS)
    owners = jax.vmap(lambda own, number: deal_out(jax.random.fold_in(part_splits[11], 2), own, number, QROWS, N_SEQ, 1, CAP, 2))(owners_keys, owners_turns).reshape((MROWS, 1))
    return dict(patches=patches, image_sizes=image_sizes, seg_ids=seg_ids, pad_mask=pad_mask, ln1_gain=ln1_gain, qkv_weight=qkv_weight, out_weight=out_weight, ln2_gain=ln2_gain, fc1_weight=fc1_weight, fc2_weight=fc2_weight, proj_weight=proj_weight, owners=owners)


EPS = 1e-06

def layer_norm(values, gain):
    mean = lax.optimization_barrier(jnp.mean(values, axis=-1, keepdims=True))
    centred = values - mean
    spread = lax.optimization_barrier(jnp.mean(centred * centred, axis=-1, keepdims=True))
    return centred * lax.rsqrt(spread + EPS) * gain

def position_table(seg_local, image_sizes, index, width):
    heights = image_sizes[:, 0]
    widths = image_sizes[:, 1]
    areas = heights * widths
    starts = jnp.cumsum(areas) - areas
    image_ids = jnp.arange(image_sizes.shape[0], dtype=jnp.int32)
    member = (seg_local[:, None] == image_ids[None, :]).astype(jnp.int32)
    begin = lax.optimization_barrier(jnp.sum(member * starts[None, :], axis=1))
    across = lax.optimization_barrier(jnp.sum(member * widths[None, :], axis=1))
    offset = index - begin
    blocks = offset // 4
    inner = offset % 4
    half = jnp.maximum(across // 2, 1)
    row_pos = (2 * (blocks // half) + inner // 2).astype(jnp.float32)
    col_pos = (2 * (blocks % half) + inner % 2).astype(jnp.float32)
    quarter = width // 4
    freq = jnp.exp(jnp.arange(quarter, dtype=jnp.float32) * (-math.log(10000.0) / quarter))
    row_angle = row_pos[:, None] * freq[None, :]
    col_angle = col_pos[:, None] * freq[None, :]
    return jnp.concatenate([jnp.sin(row_angle), jnp.cos(row_angle), jnp.sin(col_angle), jnp.cos(col_angle)], axis=1)

def reference(patches, image_sizes, seg_ids, pad_mask, ln1_gain, qkv_weight, out_weight, ln2_gain, fc1_weight, fc2_weight, proj_weight, owners):
    index = jnp.arange(TOKENS, dtype=jnp.int32)
    valid = pad_mask.astype(jnp.float32)
    x0 = patches.astype(jnp.float32) + position_table(seg_ids, image_sizes, index, D) * valid[:, None]
    h1 = layer_norm(x0, ln1_gain).astype(jnp.bfloat16)
    qkv = jnp.dot(h1, qkv_weight.reshape(D, 3 * D), preferred_element_type=jnp.float32).astype(jnp.bfloat16)
    queries = qkv[:, 0:D].reshape(TOKENS, NH, HD).transpose(1, 0, 2)
    keys = qkv[:, D:2 * D].reshape(TOKENS, NH, HD).transpose(1, 0, 2)
    values = qkv[:, 2 * D:].reshape(TOKENS, NH, HD).transpose(1, 0, 2)
    allowed = (seg_ids[:, None] == seg_ids[None, :]) & (pad_mask[None, :] == 1)
    scale = HD ** (-0.5)

    def one_head(parts):
        qh, kh, vh = parts
        scores = jnp.dot(qh, kh.T, preferred_element_type=jnp.float32) * scale
        best = lax.optimization_barrier(jnp.max(jnp.where(allowed, scores, -1e+30), axis=1, keepdims=True))
        weights = jnp.where(allowed, jnp.exp(scores - best), 0.0)
        total = lax.optimization_barrier(jnp.sum(weights, axis=1, keepdims=True))
        mixed = jnp.dot(weights.astype(jnp.bfloat16), vh, preferred_element_type=jnp.float32)
        return (mixed / jnp.maximum(total, 1.0)).astype(jnp.bfloat16)
    heads_out = lax.map(one_head, (queries, keys, values))
    attended = heads_out.transpose(1, 0, 2).reshape(TOKENS, D)
    x1 = x0 + jnp.dot(attended, out_weight, preferred_element_type=jnp.float32)
    h2 = layer_norm(x1, ln2_gain).astype(jnp.bfloat16)
    hidden = jax.nn.gelu(jnp.dot(h2, fc1_weight, preferred_element_type=jnp.float32), approximate=False).astype(jnp.bfloat16)
    layer = ((x1 + jnp.dot(hidden, fc2_weight, preferred_element_type=jnp.float32)) * valid[:, None]).astype(jnp.bfloat16)
    merged = layer.reshape(MROWS, 4 * D)
    proj = jnp.dot(merged, proj_weight, preferred_element_type=jnp.float32)
    emb = proj.astype(jnp.bfloat16)
    owner = owners[:, 0].reshape(N_TENSOR, QROWS)
    onehot = (owner[:, :, None] == jnp.arange(N_SEQ, dtype=jnp.int32)[None, None, :]).astype(jnp.int32)
    rank = jnp.cumsum(onehot, axis=1) - onehot
    slot = lax.optimization_barrier(jnp.sum(onehot * rank, axis=2))
    target = owner * CAP + slot
    place = (jnp.arange(N_SEQ * CAP, dtype=jnp.int32)[None, :, None] == target[:, None, :]).astype(jnp.float32)
    quarters = emb.reshape(N_TENSOR, QROWS, PROJ).astype(jnp.float32)
    placed = jnp.einsum('tsq,tqp->tsp', place, quarters, precision=lax.Precision.HIGHEST)
    delivered = placed.astype(jnp.bfloat16).reshape(N_TENSOR, N_SEQ, CAP, PROJ).transpose(1, 0, 2, 3)
    merged_seg = seg_ids.reshape(MROWS, 4)[:, 0]
    merged_valid = pad_mask.reshape(MROWS, 4)[:, 0]
    image_ids = jnp.arange(NIMG, dtype=jnp.int32)
    member = ((merged_seg[:, None] == image_ids[None, :]) & (merged_valid[:, None] == 1)).astype(jnp.float32)
    row_squares = lax.optimization_barrier(jnp.sum(proj * proj, axis=1))
    row_peak = lax.optimization_barrier(jnp.max(jnp.abs(proj), axis=1))
    sums = jnp.dot(row_squares, member, precision=lax.Precision.HIGHEST)
    image_peak = lax.optimization_barrier(jnp.max(jnp.where(member > 0, row_peak[:, None], 0.0), axis=0))
    counts = (image_sizes[:, 0] * image_sizes[:, 1] // 4).astype(jnp.float32)
    image_rms = jnp.sqrt(sums / (PROJ * jnp.maximum(counts, 1.0)))
    return (delivered, image_rms, image_peak)
```

```python
import math

import jax
import jax.numpy as jnp
from jax import lax
from jax.sharding import PartitionSpec as P

HD = 104
PROJ = 4096
SIDE = 32


EPS = 1e-06


def shifted(value, axis, steps):
    count = lax.axis_size(axis)
    leading, last = (max(0, -steps), min(count, count - steps))
    return lax.ppermute(value, axis, [(source, source + steps) for source in range(leading, last)])


def layer_norm(values, gain):
    mean = jnp.mean(values, axis=-1, keepdims=True)
    centred = values - mean
    spread = jnp.mean(centred * centred, axis=-1, keepdims=True)
    return centred * lax.rsqrt(spread + EPS) * gain


def position_table(seg_local, image_sizes, index, width):
    heights = image_sizes[:, 0]
    widths = image_sizes[:, 1]
    areas = heights * widths
    starts = jnp.cumsum(areas) - areas
    image_ids = jnp.arange(image_sizes.shape[0], dtype=jnp.int32)
    member = (seg_local[:, None] == image_ids[None, :]).astype(jnp.int32)
    begin = jnp.sum(member * starts[None, :], axis=1)
    across = jnp.sum(member * widths[None, :], axis=1)
    offset = index - begin
    blocks = offset // 4
    inner = offset % 4
    half = jnp.maximum(across // 2, 1)
    row_pos = jnp.clip(2 * (blocks // half) + inner // 2, 0, SIDE - 1)
    col_pos = jnp.clip(2 * (blocks % half) + inner % 2, 0, SIDE - 1)
    quarter = width // 4
    freq = jnp.exp(jnp.arange(quarter, dtype=jnp.float32) * (-math.log(10000.0) / quarter))
    angle = jnp.arange(SIDE, dtype=jnp.float32)[:, None] * freq[None, :]
    table = jnp.concatenate([jnp.sin(angle), jnp.cos(angle)], axis=1)
    return jnp.concatenate(
        [jnp.take(table, row_pos, axis=0), jnp.take(table, col_pos, axis=0)], axis=1
    )


def key_labels(block_start, tok_rows, seg_ids, pad_mask):
    total = seg_ids.shape[0]
    index = block_start + jnp.arange(tok_rows, dtype=jnp.int32)
    inside = (index >= 0) & (index < total)
    clamped = jnp.clip(block_start, 0, total - tok_rows)
    seg_part = lax.dynamic_slice_in_dim(seg_ids, clamped, tok_rows)
    mask_part = lax.dynamic_slice_in_dim(pad_mask, clamped, tok_rows)
    return (jnp.where(inside, seg_part, -1), inside & (mask_part == 1))


def local(
    patches,
    image_sizes,
    seg_ids,
    pad_mask,
    ln1_gain,
    qkv_weight,
    out_weight,
    ln2_gain,
    fc1_weight,
    fc2_weight,
    proj_weight,
    owners,
):
    tok_rows, width = patches.shape
    seq_count = lax.axis_size("seq")
    tensor_count = lax.axis_size("tensor")
    seq_rank = lax.axis_index("seq")
    tensor_rank = lax.axis_index("tensor")
    first = seq_rank * tok_rows
    index = first + jnp.arange(tok_rows, dtype=jnp.int32)
    seg_local = lax.dynamic_slice_in_dim(seg_ids, first, tok_rows)
    valid_local = lax.dynamic_slice_in_dim(pad_mask, first, tok_rows).astype(jnp.float32)
    x0 = (
        patches.astype(jnp.float32)
        + position_table(seg_local, image_sizes, index, width) * valid_local[:, None]
    )
    h1 = layer_norm(x0, ln1_gain).astype(jnp.bfloat16)
    local_width = qkv_weight.shape[2]
    heads = local_width // HD
    qkv = jnp.dot(
        h1, qkv_weight.reshape(width, 3 * local_width), preferred_element_type=jnp.float32
    )
    qkv = qkv.astype(jnp.bfloat16).reshape(tok_rows, 3, local_width)
    queries = qkv[:, 0].reshape(tok_rows, heads, HD)
    pairs = qkv[:, 1:]
    reach = min((SIDE * SIDE + tok_rows - 2) // tok_rows, seq_count - 1)
    blocks = [pairs]
    block_starts = [first]
    for step in range(1, reach + 1):
        blocks.append(shifted(pairs, "seq", step))
        block_starts.append(first - step * tok_rows)
        blocks.append(shifted(pairs, "seq", -step))
        block_starts.append(first + step * tok_rows)
    labels = [key_labels(start, tok_rows, seg_ids, pad_mask) for start in block_starts]
    key_seg = jnp.concatenate([item[0] for item in labels])
    key_ok = jnp.concatenate([item[1] for item in labels])
    gathered_pairs = jnp.concatenate(blocks, axis=0)
    keys = gathered_pairs[:, 0].reshape(-1, heads, HD)
    values = gathered_pairs[:, 1].reshape(-1, heads, HD)
    allowed = ((seg_local[:, None] == key_seg[None, :]) & key_ok[None, :])[None, :, :]
    scores = jnp.einsum("qhe,khe->hqk", queries, keys, preferred_element_type=jnp.float32) * HD ** (
        -0.5
    )
    best = jnp.max(jnp.where(allowed, scores, -1e30), axis=2, keepdims=True)
    weights = jnp.where(allowed, jnp.exp(scores - best), 0.0)
    total = jnp.sum(weights, axis=2)
    mixed = jnp.einsum(
        "hqk,khe->qhe", weights.astype(jnp.bfloat16), values, preferred_element_type=jnp.float32
    )
    attended = (
        (mixed / jnp.maximum(total, 1.0).T[:, :, None])
        .astype(jnp.bfloat16)
        .reshape(tok_rows, local_width)
    )
    partial_attn = jnp.dot(attended, out_weight, preferred_element_type=jnp.float32)
    groups = tok_rows // 4

    def pick_rows(array):
        return lax.dynamic_index_in_dim(
            array.reshape(groups, 4, -1), tensor_rank, 1, keepdims=False
        )

    valid_rows = pick_rows(valid_local[:, None])
    x1 = x0 + lax.psum(partial_attn.astype(jnp.bfloat16), "tensor").astype(jnp.float32)
    h2 = layer_norm(x1, ln2_gain).astype(jnp.bfloat16)
    hidden = jax.nn.gelu(
        jnp.dot(h2, fc1_weight, preferred_element_type=jnp.float32), approximate=False
    ).astype(jnp.bfloat16)
    mlp_out = jnp.dot(hidden, fc2_weight, preferred_element_type=jnp.float32)
    mlp_part = lax.psum_scatter(
        mlp_out.reshape(groups, 4, width).transpose(1, 0, 2).astype(jnp.bfloat16),
        "tensor",
        scatter_dimension=0,
        tiled=True,
    ).reshape(groups, width).astype(jnp.float32)
    x1_rows = pick_rows(x1)
    own_quarter = ((x1_rows + mlp_part) * valid_rows).astype(jnp.bfloat16)
    all_merged = lax.all_gather(own_quarter, "seq", axis=0, tiled=True)
    quarter_rows = all_merged.shape[0] // tensor_count
    proj_part = lax.psum_scatter(
        jnp.dot(all_merged, proj_weight, preferred_element_type=jnp.float32).astype(jnp.bfloat16),
        "tensor",
        scatter_dimension=0,
        tiled=True,
    ).astype(jnp.float32)
    row_begin = tensor_rank * quarter_rows
    merged_seg = lax.dynamic_slice_in_dim(seg_ids.reshape(-1, 4)[:, 0], row_begin, quarter_rows)
    merged_valid = lax.dynamic_slice_in_dim(pad_mask.reshape(-1, 4)[:, 0], row_begin, quarter_rows)
    image_ids = jnp.arange(image_sizes.shape[0], dtype=jnp.int32)
    member = ((merged_seg[:, None] == image_ids[None, :]) & (merged_valid[:, None] == 1)).astype(
        jnp.float32
    )
    row_squares = jnp.sum(proj_part * proj_part, axis=1)
    row_peak = jnp.max(jnp.abs(proj_part), axis=1)
    local_sums = jnp.dot(row_squares, member, precision=lax.Precision.HIGHEST)
    local_peaks = jnp.max(jnp.where(member > 0, row_peak[:, None], 0.0), axis=0)
    dp_count = lax.axis_size("dp")
    dp_rank = lax.axis_index("dp")
    slots = jnp.arange(dp_count, dtype=jnp.int32)[:, None] == dp_rank
    everyone = ("dp", "seq", "tensor")
    sums = lax.psum(jnp.where(slots, local_sums[None, :], 0.0), everyone)[dp_rank]
    image_peak = lax.pmax(jnp.where(slots, local_peaks[None, :], 0.0), everyone)[dp_rank]
    counts = (image_sizes[:, 0] * image_sizes[:, 1] // 4).astype(jnp.float32)
    image_rms = jnp.sqrt(sums / (PROJ * jnp.maximum(counts, 1.0)))
    emb = proj_part.astype(jnp.bfloat16)
    capacity = 2 * quarter_rows // seq_count
    owner_rows = lax.dynamic_slice_in_dim(owners[:, 0], row_begin, quarter_rows)
    onehot = (owner_rows[:, None] == jnp.arange(seq_count, dtype=jnp.int32)[None, :]).astype(
        jnp.int32
    )
    rank = jnp.cumsum(onehot, axis=0) - onehot
    slot = jnp.sum(onehot * rank, axis=1)
    target = owner_rows * capacity + slot
    place = (jnp.arange(seq_count * capacity, dtype=jnp.int32)[:, None] == target[None, :]).astype(
        jnp.bfloat16
    )
    buffer = jnp.dot(place, emb, preferred_element_type=jnp.float32).astype(jnp.bfloat16)
    buffer = buffer.reshape(seq_count, capacity, emb.shape[1])
    arrived = lax.all_to_all(buffer, "seq", split_axis=0, concat_axis=2, tiled=True)
    delivered = arrived.reshape(1, 1, capacity, arrived.shape[2])
    return (delivered, image_rms, image_peak)


def solution(mesh):
    in_specs = (
        P(("dp", "seq"), None),
        P("dp", None),
        P("dp"),
        P("dp"),
        P(),
        P(None, None, "tensor"),
        P("tensor", None),
        P(),
        P(None, "tensor"),
        P("tensor", None),
        P("tensor", "seq"),
        P("dp", None),
    )
    out_specs = (P(("dp", "seq"), "tensor", None, None), P("dp"), P("dp"))
    return jax.shard_map(local, mesh=mesh, in_specs=in_specs, out_specs=out_specs, check_vma=False)
```

```python
import math

import jax
import jax.numpy as jnp
from jax import lax
from jax.sharding import PartitionSpec as P

HD = 104
PROJ = 4096
SIDE = 32


EPS = 1e-06


def shifted(value, axis, steps):
    count = lax.axis_size(axis)
    leading, last = (max(0, -steps), min(count, count - steps))
    return lax.ppermute(value, axis, [(source, source + steps) for source in range(leading, last)])


def swap(value, axis, bit):
    count = lax.axis_size(axis)
    return lax.ppermute(value, axis, [(source, source ^ bit) for source in range(count)])


def take_half(value, index, axis):
    return lax.dynamic_index_in_dim(value, index, axis, keepdims=False)


def tensor_reduce_scatter(parts):
    rank = lax.axis_index("tensor")
    low, high = rank % 2, rank // 2
    quads = parts.reshape((2, 2) + parts.shape[1:])
    kept = take_half(quads, low, 1)
    sent = take_half(quads, 1 - low, 1).astype(jnp.bfloat16)
    halves = kept + swap(sent, "tensor", 1).astype(jnp.float32)
    sent = take_half(halves, 1 - high, 0).astype(jnp.bfloat16)
    return take_half(halves, high, 0) + swap(sent, "tensor", 2).astype(jnp.float32)


def tensor_all_gather(mine):
    rank = lax.axis_index("tensor")
    low, high = rank % 2, rank // 2
    other = swap(mine, "tensor", 2)
    pair = jnp.where(high == 0, jnp.stack([mine, other]), jnp.stack([other, mine]))
    other = swap(pair, "tensor", 1)
    return jnp.where(low == 0, jnp.stack([pair, other], 1), jnp.stack([other, pair], 1))


def butterfly_stats(stats):
    for axis, bits in (("tensor", (1, 2)), ("seq", (1, 2, 4))):
        for bit in bits:
            if bit < lax.axis_size(axis):
                other = swap(stats, axis, bit)
                stats = jnp.stack([stats[0] + other[0], jnp.maximum(stats[1], other[1])])
    return stats


def layer_norm(values, gain):
    mean = jnp.mean(values, axis=-1, keepdims=True)
    centred = values - mean
    spread = jnp.mean(centred * centred, axis=-1, keepdims=True)
    return centred * lax.rsqrt(spread + EPS) * gain


def position_table(seg_local, image_sizes, index, width):
    heights = image_sizes[:, 0]
    widths = image_sizes[:, 1]
    areas = heights * widths
    starts = jnp.cumsum(areas) - areas
    image_ids = jnp.arange(image_sizes.shape[0], dtype=jnp.int32)
    member = (seg_local[:, None] == image_ids[None, :]).astype(jnp.int32)
    begin = jnp.sum(member * starts[None, :], axis=1)
    across = jnp.sum(member * widths[None, :], axis=1)
    offset = index - begin
    blocks = offset // 4
    inner = offset % 4
    half = jnp.maximum(across // 2, 1)
    row_pos = jnp.clip(2 * (blocks // half) + inner // 2, 0, SIDE - 1)
    col_pos = jnp.clip(2 * (blocks % half) + inner % 2, 0, SIDE - 1)
    quarter = width // 4
    freq = jnp.exp(jnp.arange(quarter, dtype=jnp.float32) * (-math.log(10000.0) / quarter))
    angle = jnp.arange(SIDE, dtype=jnp.float32)[:, None] * freq[None, :]
    table = jnp.concatenate([jnp.sin(angle), jnp.cos(angle)], axis=1)
    return jnp.concatenate(
        [jnp.take(table, row_pos, axis=0), jnp.take(table, col_pos, axis=0)], axis=1
    )


def key_labels(block_start, tok_rows, seg_ids, pad_mask):
    total = seg_ids.shape[0]
    index = block_start + jnp.arange(tok_rows, dtype=jnp.int32)
    inside = (index >= 0) & (index < total)
    clamped = jnp.clip(block_start, 0, total - tok_rows)
    seg_part = lax.dynamic_slice_in_dim(seg_ids, clamped, tok_rows)
    mask_part = lax.dynamic_slice_in_dim(pad_mask, clamped, tok_rows)
    return (jnp.where(inside, seg_part, -1), inside & (mask_part == 1))


def local(
    patches,
    image_sizes,
    seg_ids,
    pad_mask,
    ln1_gain,
    qkv_weight,
    out_weight,
    ln2_gain,
    fc1_weight,
    fc2_weight,
    proj_weight,
    owners,
):
    tok_rows, width = patches.shape
    seq_count = lax.axis_size("seq")
    tensor_count = lax.axis_size("tensor")
    seq_rank = lax.axis_index("seq")
    tensor_rank = lax.axis_index("tensor")
    first = seq_rank * tok_rows
    index = first + jnp.arange(tok_rows, dtype=jnp.int32)
    seg_local = lax.dynamic_slice_in_dim(seg_ids, first, tok_rows)
    valid_local = lax.dynamic_slice_in_dim(pad_mask, first, tok_rows).astype(jnp.float32)
    x0 = (
        patches.astype(jnp.float32)
        + position_table(seg_local, image_sizes, index, width) * valid_local[:, None]
    )
    h1 = layer_norm(x0, ln1_gain).astype(jnp.bfloat16)
    local_width = qkv_weight.shape[2]
    heads = local_width // HD
    qkv = jnp.dot(
        h1, qkv_weight.reshape(width, 3 * local_width), preferred_element_type=jnp.float32
    )
    qkv = qkv.astype(jnp.bfloat16).reshape(tok_rows, 3, local_width)
    queries = qkv[:, 0].reshape(tok_rows, heads, HD)
    pairs = qkv[:, 1:]
    reach = min((SIDE * SIDE + tok_rows - 2) // tok_rows, seq_count - 1)
    blocks = [pairs]
    block_starts = [first]
    for step in range(1, reach + 1):
        blocks.append(shifted(pairs, "seq", step))
        block_starts.append(first - step * tok_rows)
        blocks.append(shifted(pairs, "seq", -step))
        block_starts.append(first + step * tok_rows)
    labels = [key_labels(start, tok_rows, seg_ids, pad_mask) for start in block_starts]
    key_seg = jnp.concatenate([item[0] for item in labels])
    key_ok = jnp.concatenate([item[1] for item in labels])
    gathered_pairs = jnp.concatenate(blocks, axis=0)
    keys = gathered_pairs[:, 0].reshape(-1, heads, HD)
    values = gathered_pairs[:, 1].reshape(-1, heads, HD)
    allowed = ((seg_local[:, None] == key_seg[None, :]) & key_ok[None, :])[None, :, :]
    scores = jnp.einsum("qhe,khe->hqk", queries, keys, preferred_element_type=jnp.float32) * HD ** (
        -0.5
    )
    best = jnp.max(jnp.where(allowed, scores, -1e30), axis=2, keepdims=True)
    weights = jnp.where(allowed, jnp.exp(scores - best), 0.0)
    total = jnp.sum(weights, axis=2)
    mixed = jnp.einsum(
        "hqk,khe->qhe", weights.astype(jnp.bfloat16), values, preferred_element_type=jnp.float32
    )
    attended = (
        (mixed / jnp.maximum(total, 1.0).T[:, :, None])
        .astype(jnp.bfloat16)
        .reshape(tok_rows, local_width)
    )
    partial_attn = jnp.dot(attended, out_weight, preferred_element_type=jnp.float32)
    groups = tok_rows // 4

    def pick_rows(array):
        return lax.dynamic_index_in_dim(
            array.reshape(groups, 4, -1), tensor_rank, 1, keepdims=False
        )

    valid_rows = pick_rows(valid_local[:, None])
    attn_sum = tensor_reduce_scatter(partial_attn.reshape(tensor_count, -1, width))
    attn_full = tensor_all_gather(attn_sum.astype(jnp.bfloat16)).reshape(tok_rows, width)
    x1 = x0 + attn_full.astype(jnp.float32)
    h2 = layer_norm(x1, ln2_gain).astype(jnp.bfloat16)
    hidden = jax.nn.gelu(
        jnp.dot(h2, fc1_weight, preferred_element_type=jnp.float32), approximate=False
    ).astype(jnp.bfloat16)
    mlp_out = jnp.dot(hidden, fc2_weight, preferred_element_type=jnp.float32)
    mlp_part = tensor_reduce_scatter(mlp_out.reshape(groups, 4, width).transpose(1, 0, 2))
    x1_rows = pick_rows(x1)
    own_quarter = ((x1_rows + mlp_part) * valid_rows).astype(jnp.bfloat16)
    all_merged = lax.all_gather(own_quarter, "seq", axis=0, tiled=True)
    quarter_rows = all_merged.shape[0] // tensor_count
    proj_part = lax.psum_scatter(
        jnp.dot(all_merged, proj_weight, preferred_element_type=jnp.float32).astype(jnp.bfloat16),
        "tensor",
        scatter_dimension=0,
        tiled=True,
    ).astype(jnp.float32)
    row_begin = tensor_rank * quarter_rows
    merged_seg = lax.dynamic_slice_in_dim(seg_ids.reshape(-1, 4)[:, 0], row_begin, quarter_rows)
    merged_valid = lax.dynamic_slice_in_dim(pad_mask.reshape(-1, 4)[:, 0], row_begin, quarter_rows)
    image_ids = jnp.arange(image_sizes.shape[0], dtype=jnp.int32)
    member = ((merged_seg[:, None] == image_ids[None, :]) & (merged_valid[:, None] == 1)).astype(
        jnp.float32
    )
    row_squares = jnp.sum(proj_part * proj_part, axis=1)
    row_peak = jnp.max(jnp.abs(proj_part), axis=1)
    local_sums = jnp.dot(row_squares, member, precision=lax.Precision.HIGHEST)
    local_peaks = jnp.max(jnp.where(member > 0, row_peak[:, None], 0.0), axis=0)
    stats = butterfly_stats(jnp.stack([local_sums, local_peaks]))
    sums, image_peak = stats[0], stats[1]
    counts = (image_sizes[:, 0] * image_sizes[:, 1] // 4).astype(jnp.float32)
    image_rms = jnp.sqrt(sums / (PROJ * jnp.maximum(counts, 1.0)))
    emb = proj_part.astype(jnp.bfloat16)
    capacity = 2 * quarter_rows // seq_count
    owner_rows = lax.dynamic_slice_in_dim(owners[:, 0], row_begin, quarter_rows)
    onehot = (owner_rows[:, None] == jnp.arange(seq_count, dtype=jnp.int32)[None, :]).astype(
        jnp.int32
    )
    rank = jnp.cumsum(onehot, axis=0) - onehot
    slot = jnp.sum(onehot * rank, axis=1)
    target = owner_rows * capacity + slot
    place = (jnp.arange(seq_count * capacity, dtype=jnp.int32)[:, None] == target[None, :]).astype(
        jnp.bfloat16
    )
    buffer = jnp.dot(place, emb, preferred_element_type=jnp.float32).astype(jnp.bfloat16)
    buffer = buffer.reshape(seq_count, capacity, emb.shape[1])
    arrived = lax.all_to_all(buffer, "seq", split_axis=0, concat_axis=2, tiled=True)
    delivered = arrived.reshape(1, 1, capacity, arrived.shape[2])
    return (delivered, image_rms, image_peak)


def solution(mesh):
    in_specs = (
        P(("dp", "seq"), None),
        P("dp", None),
        P("dp"),
        P("dp"),
        P(),
        P(None, None, "tensor"),
        P("tensor", None),
        P(),
        P(None, "tensor"),
        P("tensor", None),
        P("tensor", "seq"),
        P("dp", None),
    )
    out_specs = (P(("dp", "seq"), "tensor", None, None), P("dp"), P("dp"))
    return jax.shard_map(local, mesh=mesh, in_specs=in_specs, out_specs=out_specs, check_vma=False)
```

```python
import math

import jax
import jax.numpy as jnp
from jax import lax
from jax.sharding import PartitionSpec as P

HD = 104
PROJ = 4096
SIDE = 32


EPS = 1e-06


def shifted(value, axis, steps):
    count = lax.axis_size(axis)
    leading, last = (max(0, -steps), min(count, count - steps))
    return lax.ppermute(value, axis, [(source, source + steps) for source in range(leading, last)])


def swap(value, axis, bit):
    count = lax.axis_size(axis)
    return lax.ppermute(value, axis, [(source, source ^ bit) for source in range(count)])


def take_half(value, index, axis):
    return lax.dynamic_index_in_dim(value, index, axis, keepdims=False)


def tensor_reduce_scatter(parts):
    rank = lax.axis_index("tensor")
    low, high = rank % 2, rank // 2
    quads = parts.reshape((2, 2) + parts.shape[1:])
    kept = take_half(quads, low, 1)
    sent = take_half(quads, 1 - low, 1).astype(jnp.bfloat16)
    halves = kept + swap(sent, "tensor", 1).astype(jnp.float32)
    sent = take_half(halves, 1 - high, 0).astype(jnp.bfloat16)
    return take_half(halves, high, 0) + swap(sent, "tensor", 2).astype(jnp.float32)


def tensor_all_gather(mine):
    rank = lax.axis_index("tensor")
    low, high = rank % 2, rank // 2
    other = swap(mine, "tensor", 2)
    pair = jnp.where(high == 0, jnp.stack([mine, other]), jnp.stack([other, mine]))
    other = swap(pair, "tensor", 1)
    return jnp.where(low == 0, jnp.stack([pair, other], 1), jnp.stack([other, pair], 1))


def butterfly_stats(stats):
    for axis, bits in (("tensor", (1, 2)), ("seq", (1, 2, 4))):
        for bit in bits:
            if bit < lax.axis_size(axis):
                other = swap(stats, axis, bit)
                stats = jnp.stack([stats[0] + other[0], jnp.maximum(stats[1], other[1])])
    return stats


def layer_norm(values, gain):
    mean = jnp.mean(values, axis=-1, keepdims=True)
    centred = values - mean
    spread = jnp.mean(centred * centred, axis=-1, keepdims=True)
    return centred * lax.rsqrt(spread + EPS) * gain


def position_table(seg_local, image_sizes, index, width):
    heights = image_sizes[:, 0]
    widths = image_sizes[:, 1]
    areas = heights * widths
    starts = jnp.cumsum(areas) - areas
    image_ids = jnp.arange(image_sizes.shape[0], dtype=jnp.int32)
    member = (seg_local[:, None] == image_ids[None, :]).astype(jnp.int32)
    begin = jnp.sum(member * starts[None, :], axis=1)
    across = jnp.sum(member * widths[None, :], axis=1)
    offset = index - begin
    blocks = offset // 4
    inner = offset % 4
    half = jnp.maximum(across // 2, 1)
    row_pos = jnp.clip(2 * (blocks // half) + inner // 2, 0, SIDE - 1)
    col_pos = jnp.clip(2 * (blocks % half) + inner % 2, 0, SIDE - 1)
    quarter = width // 4
    freq = jnp.exp(jnp.arange(quarter, dtype=jnp.float32) * (-math.log(10000.0) / quarter))
    angle = jnp.arange(SIDE, dtype=jnp.float32)[:, None] * freq[None, :]
    table = jnp.concatenate([jnp.sin(angle), jnp.cos(angle)], axis=1)
    return jnp.concatenate(
        [jnp.take(table, row_pos, axis=0), jnp.take(table, col_pos, axis=0)], axis=1
    )


def key_labels(block_start, tok_rows, seg_ids, pad_mask):
    total = seg_ids.shape[0]
    index = block_start + jnp.arange(tok_rows, dtype=jnp.int32)
    inside = (index >= 0) & (index < total)
    clamped = jnp.clip(block_start, 0, total - tok_rows)
    seg_part = lax.dynamic_slice_in_dim(seg_ids, clamped, tok_rows)
    mask_part = lax.dynamic_slice_in_dim(pad_mask, clamped, tok_rows)
    return (jnp.where(inside, seg_part, -1), inside & (mask_part == 1))


def local(
    patches,
    image_sizes,
    seg_ids,
    pad_mask,
    ln1_gain,
    qkv_weight,
    out_weight,
    ln2_gain,
    fc1_weight,
    fc2_weight,
    proj_weight,
    owners,
):
    tok_rows, width = patches.shape
    seq_count = lax.axis_size("seq")
    tensor_count = lax.axis_size("tensor")
    seq_rank = lax.axis_index("seq")
    tensor_rank = lax.axis_index("tensor")
    first = seq_rank * tok_rows
    index = first + jnp.arange(tok_rows, dtype=jnp.int32)
    seg_local = lax.dynamic_slice_in_dim(seg_ids, first, tok_rows)
    valid_local = lax.dynamic_slice_in_dim(pad_mask, first, tok_rows).astype(jnp.float32)
    x0 = (
        patches.astype(jnp.float32)
        + position_table(seg_local, image_sizes, index, width) * valid_local[:, None]
    )
    h1 = layer_norm(x0, ln1_gain).astype(jnp.bfloat16)
    local_width = qkv_weight.shape[2]
    heads = local_width // HD
    qkv = jnp.dot(
        h1, qkv_weight.reshape(width, 3 * local_width), preferred_element_type=jnp.float32
    )
    qkv = qkv.astype(jnp.bfloat16).reshape(tok_rows, 3, local_width)
    queries = qkv[:, 0].reshape(tok_rows, heads, HD)
    pairs = qkv[:, 1:]
    reach = min((SIDE * SIDE + tok_rows - 2) // tok_rows, seq_count - 1)
    blocks = [pairs]
    block_starts = [first]
    for step in range(1, reach + 1):
        blocks.append(shifted(pairs, "seq", step))
        block_starts.append(first - step * tok_rows)
        blocks.append(shifted(pairs, "seq", -step))
        block_starts.append(first + step * tok_rows)
    labels = [key_labels(start, tok_rows, seg_ids, pad_mask) for start in block_starts]
    key_seg = jnp.concatenate([item[0] for item in labels])
    key_ok = jnp.concatenate([item[1] for item in labels])
    gathered_pairs = jnp.concatenate(blocks, axis=0)
    keys = gathered_pairs[:, 0].reshape(-1, heads, HD)
    values = gathered_pairs[:, 1].reshape(-1, heads, HD)
    allowed = ((seg_local[:, None] == key_seg[None, :]) & key_ok[None, :])[None, :, :]
    scores = jnp.einsum("qhe,khe->hqk", queries, keys, preferred_element_type=jnp.float32) * HD ** (
        -0.5
    )
    best = jnp.max(jnp.where(allowed, scores, -1e30), axis=2, keepdims=True)
    weights = jnp.where(allowed, jnp.exp(scores - best), 0.0)
    total = jnp.sum(weights, axis=2)
    mixed = jnp.einsum(
        "hqk,khe->qhe", weights.astype(jnp.bfloat16), values, preferred_element_type=jnp.float32
    )
    attended = (
        (mixed / jnp.maximum(total, 1.0).T[:, :, None])
        .astype(jnp.bfloat16)
        .reshape(tok_rows, local_width)
    )
    partial_attn = jnp.dot(attended, out_weight, preferred_element_type=jnp.float32)
    groups = tok_rows // 4

    def pick_rows(array):
        return lax.dynamic_index_in_dim(
            array.reshape(groups, 4, -1), tensor_rank, 1, keepdims=False
        )

    valid_rows = pick_rows(valid_local[:, None])
    attn_sum = tensor_reduce_scatter(partial_attn.reshape(tensor_count, -1, width))
    attn_full = tensor_all_gather(attn_sum.astype(jnp.bfloat16)).reshape(tok_rows, width)
    x1 = x0 + attn_full.astype(jnp.float32)
    h2 = layer_norm(x1, ln2_gain).astype(jnp.bfloat16)
    hidden = jax.nn.gelu(
        jnp.dot(h2, fc1_weight, preferred_element_type=jnp.float32), approximate=False
    ).astype(jnp.bfloat16)
    mlp_out = jnp.dot(hidden, fc2_weight, preferred_element_type=jnp.float32)
    mlp_part = tensor_reduce_scatter(mlp_out.reshape(groups, 4, width).transpose(1, 0, 2))
    x1_rows = pick_rows(x1)
    own_quarter = ((x1_rows + mlp_part) * valid_rows).astype(jnp.bfloat16)
    received = [own_quarter] + [swap(own_quarter, "seq", bit) for bit in range(1, seq_count)]
    gathered = jnp.stack(received).reshape(seq_count * groups, width)
    partial_proj = jnp.dot(gathered, proj_weight, preferred_element_type=jnp.float32)
    order = jnp.arange(seq_count, dtype=jnp.int32) ^ seq_rank
    partial_proj = jnp.take(partial_proj.reshape(seq_count, groups, -1), order, axis=0)
    quarter_rows = seq_count * groups // tensor_count
    proj_part = tensor_reduce_scatter(partial_proj.reshape(tensor_count, quarter_rows, -1))
    row_begin = tensor_rank * quarter_rows
    merged_seg = lax.dynamic_slice_in_dim(seg_ids.reshape(-1, 4)[:, 0], row_begin, quarter_rows)
    merged_valid = lax.dynamic_slice_in_dim(pad_mask.reshape(-1, 4)[:, 0], row_begin, quarter_rows)
    image_ids = jnp.arange(image_sizes.shape[0], dtype=jnp.int32)
    member = ((merged_seg[:, None] == image_ids[None, :]) & (merged_valid[:, None] == 1)).astype(
        jnp.float32
    )
    row_squares = jnp.sum(proj_part * proj_part, axis=1)
    row_peak = jnp.max(jnp.abs(proj_part), axis=1)
    local_sums = jnp.dot(row_squares, member, precision=lax.Precision.HIGHEST)
    local_peaks = jnp.max(jnp.where(member > 0, row_peak[:, None], 0.0), axis=0)
    stats = butterfly_stats(jnp.stack([local_sums, local_peaks]))
    sums, image_peak = stats[0], stats[1]
    counts = (image_sizes[:, 0] * image_sizes[:, 1] // 4).astype(jnp.float32)
    image_rms = jnp.sqrt(sums / (PROJ * jnp.maximum(counts, 1.0)))
    emb = proj_part.astype(jnp.bfloat16)
    capacity = 2 * quarter_rows // seq_count
    owner_rows = lax.dynamic_slice_in_dim(owners[:, 0], row_begin, quarter_rows)
    onehot = (owner_rows[:, None] == jnp.arange(seq_count, dtype=jnp.int32)[None, :]).astype(
        jnp.int32
    )
    rank = jnp.cumsum(onehot, axis=0) - onehot
    slot = jnp.sum(onehot * rank, axis=1)
    target = owner_rows * capacity + slot
    place = (jnp.arange(seq_count * capacity, dtype=jnp.int32)[:, None] == target[None, :]).astype(
        jnp.bfloat16
    )
    buffer = jnp.dot(place, emb, preferred_element_type=jnp.float32).astype(jnp.bfloat16)
    buffer = buffer.reshape(seq_count, capacity, emb.shape[1])
    arrived = lax.all_to_all(buffer, "seq", split_axis=0, concat_axis=2, tiled=True)
    delivered = arrived.reshape(1, 1, capacity, arrived.shape[2])
    return (delivered, image_rms, image_peak)


def solution(mesh):
    in_specs = (
        P(("dp", "seq"), None),
        P("dp", None),
        P("dp"),
        P("dp"),
        P(),
        P(None, None, "tensor"),
        P("tensor", None),
        P(),
        P(None, "tensor"),
        P("tensor", None),
        P("tensor", "seq"),
        P("dp", None),
    )
    out_specs = (P(("dp", "seq"), "tensor", None, None), P("dp"), P("dp"))
    return jax.shard_map(local, mesh=mesh, in_specs=in_specs, out_specs=out_specs, check_vma=False)
```

```python
import math

import jax
import jax.numpy as jnp
from jax import lax
from jax.sharding import PartitionSpec as P

HD = 104
PROJ = 4096
SIDE = 32


EPS = 1e-06


def shifted(value, axis, steps):
    count = lax.axis_size(axis)
    leading, last = (max(0, -steps), min(count, count - steps))
    return lax.ppermute(value, axis, [(source, source + steps) for source in range(leading, last)])


def swap(value, axis, bit):
    count = lax.axis_size(axis)
    return lax.ppermute(value, axis, [(source, source ^ bit) for source in range(count)])


def take_half(value, index, axis):
    return lax.dynamic_index_in_dim(value, index, axis, keepdims=False)


def tensor_reduce_scatter(parts):
    rank = lax.axis_index("tensor")
    low, high = rank % 2, rank // 2
    quads = parts.reshape((2, 2) + parts.shape[1:])
    kept = take_half(quads, low, 1)
    sent = take_half(quads, 1 - low, 1).astype(jnp.bfloat16)
    halves = kept + swap(sent, "tensor", 1).astype(jnp.float32)
    sent = take_half(halves, 1 - high, 0).astype(jnp.bfloat16)
    return take_half(halves, high, 0) + swap(sent, "tensor", 2).astype(jnp.float32)


def tensor_all_gather(mine):
    rank = lax.axis_index("tensor")
    low, high = rank % 2, rank // 2
    other = swap(mine, "tensor", 2)
    pair = jnp.where(high == 0, jnp.stack([mine, other]), jnp.stack([other, mine]))
    other = swap(pair, "tensor", 1)
    return jnp.where(low == 0, jnp.stack([pair, other], 1), jnp.stack([other, pair], 1))


def butterfly_stats(stats):
    for axis, bits in (("tensor", (1, 2)), ("seq", (1, 2, 4))):
        for bit in bits:
            if bit < lax.axis_size(axis):
                other = swap(stats, axis, bit)
                stats = jnp.stack([stats[0] + other[0], jnp.maximum(stats[1], other[1])])
    return stats


def layer_norm(values, gain):
    mean = jnp.mean(values, axis=-1, keepdims=True)
    centred = values - mean
    spread = jnp.mean(centred * centred, axis=-1, keepdims=True)
    return centred * lax.rsqrt(spread + EPS) * gain


def position_table(seg_local, image_sizes, index, width):
    heights = image_sizes[:, 0]
    widths = image_sizes[:, 1]
    areas = heights * widths
    starts = jnp.cumsum(areas) - areas
    image_ids = jnp.arange(image_sizes.shape[0], dtype=jnp.int32)
    member = (seg_local[:, None] == image_ids[None, :]).astype(jnp.int32)
    begin = jnp.sum(member * starts[None, :], axis=1)
    across = jnp.sum(member * widths[None, :], axis=1)
    offset = index - begin
    blocks = offset // 4
    inner = offset % 4
    half = jnp.maximum(across // 2, 1)
    row_pos = jnp.clip(2 * (blocks // half) + inner // 2, 0, SIDE - 1)
    col_pos = jnp.clip(2 * (blocks % half) + inner % 2, 0, SIDE - 1)
    quarter = width // 4
    freq = jnp.exp(jnp.arange(quarter, dtype=jnp.float32) * (-math.log(10000.0) / quarter))
    angle = jnp.arange(SIDE, dtype=jnp.float32)[:, None] * freq[None, :]
    table = jnp.concatenate([jnp.sin(angle), jnp.cos(angle)], axis=1)
    return jnp.concatenate(
        [jnp.take(table, row_pos, axis=0), jnp.take(table, col_pos, axis=0)], axis=1
    )


def key_labels(block_start, tok_rows, seg_ids, pad_mask):
    total = seg_ids.shape[0]
    index = block_start + jnp.arange(tok_rows, dtype=jnp.int32)
    inside = (index >= 0) & (index < total)
    clamped = jnp.clip(block_start, 0, total - tok_rows)
    seg_part = lax.dynamic_slice_in_dim(seg_ids, clamped, tok_rows)
    mask_part = lax.dynamic_slice_in_dim(pad_mask, clamped, tok_rows)
    return (jnp.where(inside, seg_part, -1), inside & (mask_part == 1))


def local(
    patches,
    image_sizes,
    seg_ids,
    pad_mask,
    ln1_gain,
    qkv_weight,
    out_weight,
    ln2_gain,
    fc1_weight,
    fc2_weight,
    proj_weight,
    owners,
):
    tok_rows, width = patches.shape
    seq_count = lax.axis_size("seq")
    tensor_count = lax.axis_size("tensor")
    seq_rank = lax.axis_index("seq")
    tensor_rank = lax.axis_index("tensor")
    first = seq_rank * tok_rows
    groups = tok_rows // 4

    def by_quarter(array):
        return jnp.swapaxes(array.reshape((groups, 4) + array.shape[1:]), 0, 1).reshape(array.shape)

    index = first + by_quarter(jnp.arange(tok_rows, dtype=jnp.int32))
    seg_local = by_quarter(lax.dynamic_slice_in_dim(seg_ids, first, tok_rows))
    valid_local = by_quarter(lax.dynamic_slice_in_dim(pad_mask, first, tok_rows)).astype(jnp.float32)
    x0 = (
        by_quarter(patches).astype(jnp.float32)
        + position_table(seg_local, image_sizes, index, width) * valid_local[:, None]
    )
    h1 = layer_norm(x0, ln1_gain).astype(jnp.bfloat16)
    local_width = qkv_weight.shape[2]
    heads = local_width // HD
    qkv = jnp.dot(
        h1, qkv_weight.reshape(width, 3 * local_width), preferred_element_type=jnp.float32
    )
    qkv = qkv.astype(jnp.bfloat16).reshape(tok_rows, 3, local_width)
    queries = qkv[:, 0].reshape(tok_rows, heads, HD)
    reach = min((SIDE * SIDE + tok_rows - 2) // tok_rows, seq_count - 1)
    steps = [0] + [sign * step for step in range(1, reach + 1) for sign in (1, -1)]
    key_blocks = [qkv[:, 1] if step == 0 else shifted(qkv[:, 1], "seq", step) for step in steps]
    value_blocks = [qkv[:, 2] if step == 0 else shifted(qkv[:, 2], "seq", step) for step in steps]
    labels = [key_labels(first - step * tok_rows, tok_rows, seg_ids, pad_mask) for step in steps]
    key_seg = jnp.concatenate([by_quarter(item[0]) for item in labels])
    key_ok = jnp.concatenate([by_quarter(item[1]) for item in labels])
    keys = jnp.concatenate(key_blocks, axis=0).reshape(-1, heads, HD)
    values = jnp.concatenate(value_blocks, axis=0).reshape(-1, heads, HD)
    allowed = ((seg_local[:, None] == key_seg[None, :]) & key_ok[None, :])[None, :, :]
    scores = jnp.einsum("qhe,khe->hqk", queries, keys, preferred_element_type=jnp.float32) * HD ** (
        -0.5
    )
    best = jnp.max(jnp.where(allowed, scores, -1e30), axis=2, keepdims=True)
    weights = jnp.where(allowed, jnp.exp(scores - best), 0.0)
    total = jnp.sum(weights, axis=2)
    mixed = jnp.einsum(
        "hqk,khe->qhe", weights.astype(jnp.bfloat16), values, preferred_element_type=jnp.float32
    )
    attended = (
        (mixed / jnp.maximum(total, 1.0).T[:, :, None])
        .astype(jnp.bfloat16)
        .reshape(tok_rows, local_width)
    )
    partial_attn = jnp.dot(attended, out_weight, preferred_element_type=jnp.float32)
    def pick_rows(array):
        return lax.dynamic_slice_in_dim(array, tensor_rank * groups, groups)

    valid_rows = pick_rows(valid_local[:, None])
    attn_sum = tensor_reduce_scatter(partial_attn.reshape(tensor_count, -1, width))
    attn_full = tensor_all_gather(attn_sum.astype(jnp.bfloat16)).reshape(tok_rows, width)
    x1 = x0 + attn_full.astype(jnp.float32)
    h2 = layer_norm(x1, ln2_gain).astype(jnp.bfloat16)
    hidden = jax.nn.gelu(
        jnp.dot(h2, fc1_weight, preferred_element_type=jnp.float32), approximate=False
    ).astype(jnp.bfloat16)
    mlp_out = jnp.dot(hidden, fc2_weight, preferred_element_type=jnp.float32)
    mlp_part = tensor_reduce_scatter(mlp_out.reshape(tensor_count, groups, width))
    x1_rows = pick_rows(x1)
    own_quarter = ((x1_rows + mlp_part) * valid_rows).astype(jnp.bfloat16)
    received = [own_quarter] + [swap(own_quarter, "seq", bit) for bit in range(1, seq_count)]
    gathered = jnp.stack(received).reshape(seq_count * groups, width)
    partial_proj = jnp.dot(gathered, proj_weight, preferred_element_type=jnp.float32)
    order = jnp.arange(seq_count, dtype=jnp.int32) ^ seq_rank
    partial_proj = jnp.take(partial_proj.reshape(seq_count, groups, -1), order, axis=0)
    quarter_rows = seq_count * groups // tensor_count
    proj_part = tensor_reduce_scatter(partial_proj.reshape(tensor_count, quarter_rows, -1))
    row_begin = tensor_rank * quarter_rows
    merged_seg = lax.dynamic_slice_in_dim(seg_ids.reshape(-1, 4)[:, 0], row_begin, quarter_rows)
    merged_valid = lax.dynamic_slice_in_dim(pad_mask.reshape(-1, 4)[:, 0], row_begin, quarter_rows)
    image_ids = jnp.arange(image_sizes.shape[0], dtype=jnp.int32)
    member = ((merged_seg[:, None] == image_ids[None, :]) & (merged_valid[:, None] == 1)).astype(
        jnp.float32
    )
    row_squares = jnp.sum(proj_part * proj_part, axis=1)
    row_peak = jnp.max(jnp.abs(proj_part), axis=1)
    local_sums = jnp.dot(row_squares, member, precision=lax.Precision.HIGHEST)
    local_peaks = jnp.max(jnp.where(member > 0, row_peak[:, None], 0.0), axis=0)
    stats = butterfly_stats(jnp.stack([local_sums, local_peaks]))
    sums, image_peak = stats[0], stats[1]
    counts = (image_sizes[:, 0] * image_sizes[:, 1] // 4).astype(jnp.float32)
    image_rms = jnp.sqrt(sums / (PROJ * jnp.maximum(counts, 1.0)))
    emb = proj_part.astype(jnp.bfloat16)
    capacity = 2 * quarter_rows // seq_count
    owner_rows = lax.dynamic_slice_in_dim(owners[:, 0], row_begin, quarter_rows)
    onehot = (owner_rows[:, None] == jnp.arange(seq_count, dtype=jnp.int32)[None, :]).astype(
        jnp.int32
    )
    rank = jnp.cumsum(onehot, axis=0) - onehot
    slot = jnp.sum(onehot * rank, axis=1)
    target = owner_rows * capacity + slot
    place = (jnp.arange(seq_count * capacity, dtype=jnp.int32)[:, None] == target[None, :]).astype(
        jnp.bfloat16
    )
    buffer = jnp.dot(place, emb, preferred_element_type=jnp.float32).astype(jnp.bfloat16)
    buffer = buffer.reshape(seq_count, capacity, emb.shape[1])
    arrived = lax.all_to_all(buffer, "seq", split_axis=0, concat_axis=2, tiled=True)
    delivered = arrived.reshape(1, 1, capacity, arrived.shape[2])
    return (delivered, image_rms, image_peak)


def solution(mesh):
    in_specs = (
        P(("dp", "seq"), None),
        P("dp", None),
        P("dp"),
        P("dp"),
        P(),
        P(None, None, "tensor"),
        P("tensor", None),
        P(),
        P(None, "tensor"),
        P("tensor", None),
        P("tensor", "seq"),
        P("dp", None),
    )
    out_specs = (P(("dp", "seq"), "tensor", None, None), P("dp"), P("dp"))
    return jax.shard_map(local, mesh=mesh, in_specs=in_specs, out_specs=out_specs, check_vma=False)
```

```python
import math

import jax
import numpy as np
import jax.numpy as jnp
from jax import lax
from jax.sharding import PartitionSpec as P

HD = 104
PROJ = 4096
SIDE = 32


EPS = 1e-06


def shifted(value, axis, steps):
    count = lax.axis_size(axis)
    leading, last = (max(0, -steps), min(count, count - steps))
    return lax.ppermute(value, axis, [(source, source + steps) for source in range(leading, last)])


def swap(value, axis, bit):
    count = lax.axis_size(axis)
    return lax.ppermute(value, axis, [(source, source ^ bit) for source in range(count)])


def take_half(value, index, axis):
    return lax.dynamic_index_in_dim(value, index, axis, keepdims=False)


def tensor_reduce_scatter(parts, rank=None):
    if rank is None:
        rank = lax.axis_index("tensor")
    low, high = rank % 2, rank // 2
    quads = parts.reshape((2, 2) + parts.shape[1:])
    kept = take_half(quads, low, 1)
    sent = take_half(quads, 1 - low, 1).astype(jnp.bfloat16)
    halves = kept + swap(sent, "tensor", 1).astype(jnp.float32)
    sent = take_half(halves, 1 - high, 0).astype(jnp.bfloat16)
    return take_half(halves, high, 0) + swap(sent, "tensor", 2).astype(jnp.float32)


def tensor_all_gather(mine):
    rank = lax.axis_index("tensor")
    low, high = rank % 2, rank // 2
    other = swap(mine, "tensor", 2)
    pair = jnp.where(high == 0, jnp.stack([mine, other]), jnp.stack([other, mine]))
    other = swap(pair, "tensor", 1)
    return jnp.where(low == 0, jnp.stack([pair, other], 1), jnp.stack([other, pair], 1))


def butterfly_stats(stats):
    for axis, bits in (("tensor", (1, 2)), ("seq", (1, 2, 4))):
        for bit in bits:
            if bit < lax.axis_size(axis):
                other = swap(stats, axis, bit)
                stats = jnp.stack([stats[0] + other[0], jnp.maximum(stats[1], other[1])])
    return stats


def layer_norm(values, gain):
    mean = jnp.mean(values, axis=-1, keepdims=True)
    centred = values - mean
    spread = jnp.mean(centred * centred, axis=-1, keepdims=True)
    return centred * lax.rsqrt(spread + EPS) * gain


def position_table(seg_local, image_sizes, index, width):
    heights = image_sizes[:, 0]
    widths = image_sizes[:, 1]
    areas = heights * widths
    starts = jnp.cumsum(areas) - areas
    image_ids = jnp.arange(image_sizes.shape[0], dtype=jnp.int32)
    member = (seg_local[:, None] == image_ids[None, :]).astype(jnp.int32)
    begin = jnp.sum(member * starts[None, :], axis=1)
    across = jnp.sum(member * widths[None, :], axis=1)
    offset = index - begin
    blocks = offset // 4
    inner = offset % 4
    half = jnp.maximum(across // 2, 1)
    row_pos = jnp.clip(2 * (blocks // half) + inner // 2, 0, SIDE - 1)
    col_pos = jnp.clip(2 * (blocks % half) + inner % 2, 0, SIDE - 1)
    quarter = width // 4
    freq = jnp.exp(jnp.arange(quarter, dtype=jnp.float32) * (-math.log(10000.0) / quarter))
    angle = jnp.arange(SIDE, dtype=jnp.float32)[:, None] * freq[None, :]
    table = jnp.concatenate([jnp.sin(angle), jnp.cos(angle)], axis=1)
    return jnp.concatenate(
        [jnp.take(table, row_pos, axis=0, mode="clip"), jnp.take(table, col_pos, axis=0, mode="clip")],
        axis=1,
    )


def key_labels(block_start, tok_rows, seg_ids, pad_mask):
    total = seg_ids.shape[0]
    index = block_start + jnp.arange(tok_rows, dtype=jnp.int32)
    inside = (index >= 0) & (index < total)
    clamped = jnp.clip(block_start, 0, total - tok_rows)
    seg_part = lax.dynamic_slice_in_dim(seg_ids, clamped, tok_rows)
    mask_part = lax.dynamic_slice_in_dim(pad_mask, clamped, tok_rows)
    return (jnp.where(inside, seg_part, -1), inside & (mask_part == 1))


def local(
    patches,
    image_sizes,
    seg_ids,
    pad_mask,
    ln1_gain,
    qkv_weight,
    out_weight,
    ln2_gain,
    fc1_weight,
    fc2_weight,
    proj_weight,
    owners,
):
    tok_rows, width = patches.shape
    seq_count = lax.axis_size("seq")
    tensor_count = lax.axis_size("tensor")
    seq_rank = lax.axis_index("seq")
    tensor_rank = lax.axis_index("tensor")
    first = seq_rank * tok_rows
    index = first + jnp.arange(tok_rows, dtype=jnp.int32)
    seg_local = lax.dynamic_slice_in_dim(seg_ids, first, tok_rows)
    valid_local = lax.dynamic_slice_in_dim(pad_mask, first, tok_rows).astype(jnp.float32)
    x0 = (
        patches.astype(jnp.float32)
        + position_table(seg_local, image_sizes, index, width) * valid_local[:, None]
    )
    h1 = layer_norm(x0, ln1_gain).astype(jnp.bfloat16)
    local_width = qkv_weight.shape[2]
    heads = local_width // HD
    qkv = jnp.dot(
        h1, qkv_weight.reshape(width, 3 * local_width), preferred_element_type=jnp.float32
    )
    qkv = qkv.astype(jnp.bfloat16).reshape(tok_rows, 3, local_width)
    queries = qkv[:, 0].reshape(tok_rows, heads, HD)
    pairs = qkv[:, 1:]
    reach = min((SIDE * SIDE + tok_rows - 2) // tok_rows, seq_count - 1)
    blocks = [pairs]
    block_starts = [first]
    for step in range(1, reach + 1):
        blocks.append(shifted(pairs, "seq", step))
        block_starts.append(first - step * tok_rows)
        blocks.append(shifted(pairs, "seq", -step))
        block_starts.append(first + step * tok_rows)
    labels = [key_labels(start, tok_rows, seg_ids, pad_mask) for start in block_starts]
    key_seg = jnp.concatenate([item[0] for item in labels])
    key_ok = jnp.concatenate([item[1] for item in labels])
    gathered_pairs = jnp.concatenate(blocks, axis=0)
    keys = gathered_pairs[:, 0].reshape(-1, heads, HD)
    values = gathered_pairs[:, 1].reshape(-1, heads, HD)
    allowed = ((seg_local[:, None] == key_seg[None, :]) & key_ok[None, :])[None, :, :]
    scores = jnp.einsum("qhe,khe->hqk", queries, keys, preferred_element_type=jnp.float32) * HD ** (
        -0.5
    )
    best = jnp.max(jnp.where(allowed, scores, -1e30), axis=2, keepdims=True)
    weights = jnp.where(allowed, jnp.exp(scores - best), 0.0)
    total = jnp.sum(weights, axis=2)
    mixed = jnp.einsum(
        "hqk,khe->qhe", weights.astype(jnp.bfloat16), values, preferred_element_type=jnp.float32
    )
    attended = (
        (mixed / jnp.maximum(total, 1.0).T[:, :, None])
        .astype(jnp.bfloat16)
        .reshape(tok_rows, local_width)
    )
    groups = tok_rows // 4
    rows = np.arange(tok_rows)
    quarter_order = jnp.asarray((rows % groups) * 4 + rows // groups, dtype=jnp.int32)

    def by_quarter(array):
        return jnp.take(array, quarter_order, axis=0, mode="clip")

    partial_attn = jnp.dot(by_quarter(attended), out_weight, preferred_element_type=jnp.float32)

    def pick_rows(array):
        return lax.dynamic_slice_in_dim(array, tensor_rank * groups, groups)

    valid_rows = pick_rows(by_quarter(valid_local)[:, None])
    attn_sum = tensor_reduce_scatter(partial_attn.reshape(tensor_count, -1, width))
    attn_full = tensor_all_gather(attn_sum.astype(jnp.bfloat16)).reshape(tok_rows, width)
    x1 = by_quarter(x0) + attn_full.astype(jnp.float32)
    h2 = layer_norm(x1, ln2_gain).astype(jnp.bfloat16)
    hidden = jax.nn.gelu(
        jnp.dot(h2, fc1_weight, preferred_element_type=jnp.float32), approximate=False
    ).astype(jnp.bfloat16)
    mlp_out = jnp.dot(hidden, fc2_weight, preferred_element_type=jnp.float32)
    mlp_part = tensor_reduce_scatter(mlp_out.reshape(tensor_count, groups, width))
    x1_rows = pick_rows(x1)
    own_quarter = ((x1_rows + mlp_part) * valid_rows).astype(jnp.bfloat16)
    received = [own_quarter] + [swap(own_quarter, "seq", bit) for bit in range(1, seq_count)]
    gathered = jnp.stack(received).reshape(seq_count * groups, width)
    partial_proj = jnp.dot(gathered, proj_weight, preferred_element_type=jnp.float32)
    quarter_rows = seq_count * groups // tensor_count
    per_quarter = seq_count // tensor_count
    proj_part = tensor_reduce_scatter(
        partial_proj.reshape(tensor_count, quarter_rows, -1), tensor_rank ^ (seq_rank // per_quarter)
    )
    row_begin = tensor_rank * quarter_rows
    local_order = jnp.arange(quarter_rows, dtype=jnp.int32) ^ ((seq_rank % per_quarter) * groups)
    merged_seg = jnp.take(seg_ids.reshape(-1, 4)[:, 0], row_begin + local_order, mode="clip")
    merged_valid = jnp.take(pad_mask.reshape(-1, 4)[:, 0], row_begin + local_order, mode="clip")
    image_ids = jnp.arange(image_sizes.shape[0], dtype=jnp.int32)
    member = ((merged_seg[:, None] == image_ids[None, :]) & (merged_valid[:, None] == 1)).astype(
        jnp.float32
    )
    row_squares = jnp.sum(proj_part * proj_part, axis=1)
    row_peak = jnp.max(jnp.abs(proj_part), axis=1)
    local_sums = jnp.dot(row_squares, member, precision=lax.Precision.HIGHEST)
    local_peaks = jnp.max(jnp.where(member > 0, row_peak[:, None], 0.0), axis=0)
    stats = butterfly_stats(jnp.stack([local_sums, local_peaks]))
    sums, image_peak = stats[0], stats[1]
    counts = (image_sizes[:, 0] * image_sizes[:, 1] // 4).astype(jnp.float32)
    image_rms = jnp.sqrt(sums / (PROJ * jnp.maximum(counts, 1.0)))
    emb = proj_part.astype(jnp.bfloat16)
    capacity = 2 * quarter_rows // seq_count
    owner_rows = lax.dynamic_slice_in_dim(owners[:, 0], row_begin, quarter_rows)
    onehot = (owner_rows[:, None] == jnp.arange(seq_count, dtype=jnp.int32)[None, :]).astype(
        jnp.int32
    )
    rank = jnp.cumsum(onehot, axis=0) - onehot
    slot = jnp.sum(onehot * rank, axis=1)
    target = jnp.take(owner_rows * capacity + slot, local_order, mode="clip")
    place = (jnp.arange(seq_count * capacity, dtype=jnp.int32)[:, None] == target[None, :]).astype(
        jnp.bfloat16
    )
    buffer = jnp.dot(place, emb, preferred_element_type=jnp.float32).astype(jnp.bfloat16)
    buffer = buffer.reshape(seq_count, capacity, emb.shape[1])
    arrived = lax.all_to_all(buffer, "seq", split_axis=0, concat_axis=2, tiled=True)
    delivered = arrived.reshape(1, 1, capacity, arrived.shape[2])
    return (delivered, image_rms, image_peak)


def solution(mesh):
    in_specs = (
        P(("dp", "seq"), None),
        P("dp", None),
        P("dp"),
        P("dp"),
        P(),
        P(None, None, "tensor"),
        P("tensor", None),
        P(),
        P(None, "tensor"),
        P("tensor", None),
        P("tensor", "seq"),
        P("dp", None),
    )
    out_specs = (P(("dp", "seq"), "tensor", None, None), P("dp"), P("dp"))
    return jax.shard_map(local, mesh=mesh, in_specs=in_specs, out_specs=out_specs, check_vma=False)
```

```python
import math

import jax
import numpy as np
import jax.numpy as jnp
from jax import lax
from jax.sharding import PartitionSpec as P

HD = 104
PROJ = 4096
SIDE = 32


EPS = 1e-06


def shifted(value, axis, steps):
    count = lax.axis_size(axis)
    leading, last = (max(0, -steps), min(count, count - steps))
    return lax.ppermute(value, axis, [(source, source + steps) for source in range(leading, last)])


def swap(value, axis, bit):
    count = lax.axis_size(axis)
    return lax.ppermute(value, axis, [(source, source ^ bit) for source in range(count)])


def take_half(value, index, axis):
    return lax.dynamic_index_in_dim(value, index, axis, keepdims=False)


def tensor_reduce_scatter(parts, rank=None):
    if rank is None:
        rank = lax.axis_index("tensor")
    low, high = rank % 2, rank // 2
    quads = parts.reshape((2, 2) + parts.shape[1:])
    kept = take_half(quads, low, 1)
    sent = take_half(quads, 1 - low, 1).astype(jnp.bfloat16)
    halves = kept + swap(sent, "tensor", 1).astype(jnp.float32)
    sent = take_half(halves, 1 - high, 0).astype(jnp.bfloat16)
    return take_half(halves, high, 0) + swap(sent, "tensor", 2).astype(jnp.float32)


def tensor_all_gather(mine):
    rank = lax.axis_index("tensor")
    low, high = rank % 2, rank // 2
    other = swap(mine, "tensor", 2)
    pair = jnp.where(high == 0, jnp.stack([mine, other]), jnp.stack([other, mine]))
    other = swap(pair, "tensor", 1)
    return jnp.where(low == 0, jnp.stack([pair, other], 1), jnp.stack([other, pair], 1))


def butterfly_stats(stats):
    for axis, bits in (("tensor", (1, 2)), ("seq", (1, 2, 4))):
        for bit in bits:
            if bit < lax.axis_size(axis):
                other = swap(stats, axis, bit)
                stats = jnp.stack([stats[0] + other[0], jnp.maximum(stats[1], other[1])])
    return stats


def layer_norm(values, gain):
    mean = jnp.mean(values, axis=-1, keepdims=True)
    centred = values - mean
    spread = jnp.mean(centred * centred, axis=-1, keepdims=True)
    return centred * lax.rsqrt(spread + EPS) * gain


def position_table(seg_local, image_sizes, index, width):
    heights = image_sizes[:, 0]
    widths = image_sizes[:, 1]
    areas = heights * widths
    starts = jnp.cumsum(areas) - areas
    image_ids = jnp.arange(image_sizes.shape[0], dtype=jnp.int32)
    member = (seg_local[:, None] == image_ids[None, :]).astype(jnp.int32)
    begin = jnp.sum(member * starts[None, :], axis=1)
    across = jnp.sum(member * widths[None, :], axis=1)
    offset = index - begin
    blocks = offset // 4
    inner = offset % 4
    half = jnp.maximum(across // 2, 1)
    row_pos = jnp.clip(2 * (blocks // half) + inner // 2, 0, SIDE - 1)
    col_pos = jnp.clip(2 * (blocks % half) + inner % 2, 0, SIDE - 1)
    quarter = width // 4
    freq = jnp.exp(jnp.arange(quarter, dtype=jnp.float32) * (-math.log(10000.0) / quarter))
    angle = jnp.arange(SIDE, dtype=jnp.float32)[:, None] * freq[None, :]
    table = jnp.concatenate([jnp.sin(angle), jnp.cos(angle)], axis=1)
    return jnp.concatenate(
        [jnp.take(table, row_pos, axis=0, mode="clip"), jnp.take(table, col_pos, axis=0, mode="clip")],
        axis=1,
    )


def key_labels(block_start, tok_rows, seg_ids, pad_mask):
    total = seg_ids.shape[0]
    index = block_start + jnp.arange(tok_rows, dtype=jnp.int32)
    inside = (index >= 0) & (index < total)
    clamped = jnp.clip(block_start, 0, total - tok_rows)
    seg_part = lax.dynamic_slice_in_dim(seg_ids, clamped, tok_rows)
    mask_part = lax.dynamic_slice_in_dim(pad_mask, clamped, tok_rows)
    return (jnp.where(inside, seg_part, -1), inside & (mask_part == 1))


def local(
    patches,
    image_sizes,
    seg_ids,
    pad_mask,
    ln1_gain,
    qkv_weight,
    out_weight,
    ln2_gain,
    fc1_weight,
    fc2_weight,
    proj_weight,
    owners,
):
    tok_rows, width = patches.shape
    seq_count = lax.axis_size("seq")
    tensor_count = lax.axis_size("tensor")
    seq_rank = lax.axis_index("seq")
    tensor_rank = lax.axis_index("tensor")
    first = seq_rank * tok_rows
    index = first + jnp.arange(tok_rows, dtype=jnp.int32)
    seg_local = lax.dynamic_slice_in_dim(seg_ids, first, tok_rows)
    valid_local = lax.dynamic_slice_in_dim(pad_mask, first, tok_rows).astype(jnp.float32)
    x0 = (
        patches.astype(jnp.float32)
        + position_table(seg_local, image_sizes, index, width) * valid_local[:, None]
    )
    h1 = layer_norm(x0, ln1_gain).astype(jnp.bfloat16)
    local_width = qkv_weight.shape[2]
    heads = local_width // HD
    qkv = jnp.dot(
        h1, qkv_weight.reshape(width, 3 * local_width), preferred_element_type=jnp.float32
    )
    qkv = qkv.astype(jnp.bfloat16).reshape(tok_rows, 3, local_width)
    queries = qkv[:, 0].reshape(tok_rows, heads, HD)
    pairs = qkv[:, 1:]
    reach = min((SIDE * SIDE + tok_rows - 2) // tok_rows, seq_count - 1)
    blocks = [pairs]
    block_starts = [first]
    for step in range(1, reach + 1):
        blocks.append(shifted(pairs, "seq", step))
        block_starts.append(first - step * tok_rows)
        blocks.append(shifted(pairs, "seq", -step))
        block_starts.append(first + step * tok_rows)
    labels = [key_labels(start, tok_rows, seg_ids, pad_mask) for start in block_starts]
    key_seg = jnp.concatenate([item[0] for item in labels])
    key_ok = jnp.concatenate([item[1] for item in labels])
    gathered_pairs = jnp.concatenate(blocks, axis=0)
    keys = gathered_pairs[:, 0].reshape(-1, heads, HD)
    values = gathered_pairs[:, 1].reshape(-1, heads, HD)
    allowed = ((seg_local[:, None] == key_seg[None, :]) & key_ok[None, :])[None, :, :]
    scores = jnp.einsum("qhe,khe->hqk", queries, keys, preferred_element_type=jnp.float32) * HD ** (
        -0.5
    )
    best = jnp.max(jnp.where(allowed, scores, -1e30), axis=2, keepdims=True)
    weights = jnp.where(allowed, jnp.exp(scores - best), 0.0)
    total = jnp.sum(weights, axis=2)
    mixed = jnp.einsum(
        "hqk,khe->qhe", weights.astype(jnp.bfloat16), values, preferred_element_type=jnp.float32
    )
    attended = (
        (mixed / jnp.maximum(total, 1.0).T[:, :, None])
        .astype(jnp.bfloat16)
        .reshape(tok_rows, local_width)
    )
    groups = tok_rows // 4
    rows = np.arange(tok_rows)
    quarter_order = jnp.asarray((rows % groups) * 4 + rows // groups, dtype=jnp.int32)

    def by_quarter(array):
        return jnp.take(array, quarter_order, axis=0, mode="clip")

    partial_attn = jnp.dot(by_quarter(attended), out_weight, preferred_element_type=jnp.float32)

    def pick_rows(array):
        return lax.dynamic_slice_in_dim(array, tensor_rank * groups, groups)

    valid_rows = pick_rows(by_quarter(valid_local)[:, None])
    attn_sum = tensor_reduce_scatter(partial_attn.reshape(tensor_count, -1, width))
    attn_full = tensor_all_gather(attn_sum.astype(jnp.bfloat16)).reshape(tok_rows, width)
    x1 = by_quarter(x0) + attn_full.astype(jnp.float32)
    h2 = layer_norm(x1, ln2_gain).astype(jnp.bfloat16)
    hidden = jax.nn.gelu(
        jnp.dot(h2, fc1_weight, preferred_element_type=jnp.float32), approximate=False
    ).astype(jnp.bfloat16)
    mlp_out = jnp.dot(hidden, fc2_weight, preferred_element_type=jnp.float32)
    mlp_part = tensor_reduce_scatter(mlp_out.reshape(tensor_count, groups, width))
    x1_rows = pick_rows(x1)
    own_quarter = ((x1_rows + mlp_part) * valid_rows).astype(jnp.bfloat16)
    received = [own_quarter] + [swap(own_quarter, "seq", bit) for bit in range(1, seq_count)]
    gathered = jnp.stack(received).reshape(seq_count * groups, width)
    partial_proj = jnp.dot(gathered, proj_weight, preferred_element_type=jnp.float32)
    quarter_rows = seq_count * groups // tensor_count
    per_quarter = seq_count // tensor_count
    proj_part = tensor_reduce_scatter(
        partial_proj.reshape(tensor_count, quarter_rows, -1), tensor_rank ^ (seq_rank // per_quarter)
    )
    row_begin = tensor_rank * quarter_rows
    local_order = jnp.arange(quarter_rows, dtype=jnp.int32) ^ ((seq_rank % per_quarter) * groups)
    merged_seg = jnp.take(seg_ids.reshape(-1, 4)[:, 0], row_begin + local_order, mode="clip")
    merged_valid = jnp.take(pad_mask.reshape(-1, 4)[:, 0], row_begin + local_order, mode="clip")
    image_ids = jnp.arange(image_sizes.shape[0], dtype=jnp.int32)
    member = ((merged_seg[:, None] == image_ids[None, :]) & (merged_valid[:, None] == 1)).astype(
        jnp.float32
    )
    row_squares = jnp.sum(proj_part * proj_part, axis=1)
    row_peak = jnp.max(jnp.abs(proj_part), axis=1)
    local_sums = jnp.dot(row_squares, member, precision=lax.Precision.HIGHEST)
    local_peaks = jnp.max(jnp.where(member > 0, row_peak[:, None], 0.0), axis=0)
    emb = proj_part.astype(jnp.bfloat16)
    capacity = 2 * quarter_rows // seq_count
    owner_rows = lax.dynamic_slice_in_dim(owners[:, 0], row_begin, quarter_rows)
    onehot = (owner_rows[:, None] == jnp.arange(seq_count, dtype=jnp.int32)[None, :]).astype(
        jnp.int32
    )
    rank = jnp.cumsum(onehot, axis=0) - onehot
    slot = jnp.sum(onehot * rank, axis=1)
    target = jnp.take(owner_rows * capacity + slot, local_order, mode="clip")
    place = (jnp.arange(seq_count * capacity, dtype=jnp.int32)[:, None] == target[None, :]).astype(
        jnp.bfloat16
    )
    buffer = jnp.dot(place, emb, preferred_element_type=jnp.float32).astype(jnp.bfloat16)
    buffer = buffer.reshape(seq_count, capacity, emb.shape[1])
    stats = jnp.stack([local_sums, local_peaks]).reshape(-1)
    high = stats.astype(jnp.bfloat16)
    low = (stats - high.astype(jnp.float32)).astype(jnp.bfloat16)
    extra = jnp.zeros((8, emb.shape[1]), jnp.bfloat16)
    extra = extra.at[0, : stats.shape[0]].set(high).at[1, : stats.shape[0]].set(low)
    buffer = jnp.concatenate([buffer, jnp.broadcast_to(extra, (seq_count,) + extra.shape)], axis=1)
    arrived = lax.all_to_all(buffer, "seq", split_axis=0, concat_axis=2, tiled=True)
    delivered = arrived[:, :capacity].reshape(1, 1, capacity, arrived.shape[2])
    parts = arrived[0, capacity : capacity + 2].reshape(2, seq_count, emb.shape[1])
    parts = parts[:, :, : stats.shape[0]].astype(jnp.float32)
    parts = (parts[0] + parts[1]).reshape(seq_count, 2, -1)
    stats = jnp.stack([jnp.sum(parts[:, 0], axis=0), jnp.max(parts[:, 1], axis=0)])
    for bit in (1, 2):
        if bit < tensor_count:
            other = swap(stats, "tensor", bit)
            stats = jnp.stack([stats[0] + other[0], jnp.maximum(stats[1], other[1])])
    sums, image_peak = stats[0], stats[1]
    counts = (image_sizes[:, 0] * image_sizes[:, 1] // 4).astype(jnp.float32)
    image_rms = jnp.sqrt(sums / (PROJ * jnp.maximum(counts, 1.0)))
    return (delivered, image_rms, image_peak)


def solution(mesh):
    in_specs = (
        P(("dp", "seq"), None),
        P("dp", None),
        P("dp"),
        P("dp"),
        P(),
        P(None, None, "tensor"),
        P("tensor", None),
        P(),
        P(None, "tensor"),
        P("tensor", None),
        P("tensor", "seq"),
        P("dp", None),
    )
    out_specs = (P(("dp", "seq"), "tensor", None, None), P("dp"), P("dp"))
    return jax.shard_map(local, mesh=mesh, in_specs=in_specs, out_specs=out_specs, check_vma=False)
```

```python
import math

import jax
import numpy as np
import jax.numpy as jnp
from jax import lax
from jax.sharding import PartitionSpec as P

HD = 104
PROJ = 4096
SIDE = 32


EPS = 1e-06


def shifted(value, axis, steps):
    count = lax.axis_size(axis)
    leading, last = (max(0, -steps), min(count, count - steps))
    return lax.ppermute(value, axis, [(source, source + steps) for source in range(leading, last)])


def swap(value, axis, bit):
    count = lax.axis_size(axis)
    return lax.ppermute(value, axis, [(source, source ^ bit) for source in range(count)])


def take_half(value, index, axis):
    return lax.dynamic_index_in_dim(value, index, axis, keepdims=False)


def tensor_reduce_scatter(parts, rank=None):
    if rank is None:
        rank = lax.axis_index("tensor")
    low, high = rank % 2, rank // 2
    quads = parts.reshape((2, 2) + parts.shape[1:])
    kept = take_half(quads, low, 1)
    sent = take_half(quads, 1 - low, 1).astype(jnp.bfloat16)
    halves = kept + swap(sent, "tensor", 1).astype(jnp.float32)
    sent = take_half(halves, 1 - high, 0).astype(jnp.bfloat16)
    return take_half(halves, high, 0) + swap(sent, "tensor", 2).astype(jnp.float32)


def tensor_all_gather(mine):
    rank = lax.axis_index("tensor")
    low, high = rank % 2, rank // 2
    other = swap(mine, "tensor", 2)
    pair = jnp.where(high == 0, jnp.stack([mine, other]), jnp.stack([other, mine]))
    other = swap(pair, "tensor", 1)
    return jnp.where(low == 0, jnp.stack([pair, other], 1), jnp.stack([other, pair], 1))


def butterfly_stats(stats):
    for axis, bits in (("tensor", (1, 2)), ("seq", (1, 2, 4))):
        for bit in bits:
            if bit < lax.axis_size(axis):
                other = swap(stats, axis, bit)
                stats = jnp.stack([stats[0] + other[0], jnp.maximum(stats[1], other[1])])
    return stats


def layer_norm(values, gain):
    mean = jnp.mean(values, axis=-1, keepdims=True)
    centred = values - mean
    spread = jnp.mean(centred * centred, axis=-1, keepdims=True)
    return centred * lax.rsqrt(spread + EPS) * gain


def position_table(seg_local, image_sizes, index, width):
    heights = image_sizes[:, 0]
    widths = image_sizes[:, 1]
    areas = heights * widths
    starts = jnp.cumsum(areas) - areas
    image_ids = jnp.arange(image_sizes.shape[0], dtype=jnp.int32)
    member = (seg_local[:, None] == image_ids[None, :]).astype(jnp.int32)
    begin = jnp.sum(member * starts[None, :], axis=1)
    across = jnp.sum(member * widths[None, :], axis=1)
    offset = index - begin
    blocks = offset // 4
    inner = offset % 4
    half = jnp.maximum(across // 2, 1)
    row_pos = jnp.clip(2 * (blocks // half) + inner // 2, 0, SIDE - 1)
    col_pos = jnp.clip(2 * (blocks % half) + inner % 2, 0, SIDE - 1)
    quarter = width // 4
    freq = jnp.exp(jnp.arange(quarter, dtype=jnp.float32) * (-math.log(10000.0) / quarter))
    angle = jnp.arange(SIDE, dtype=jnp.float32)[:, None] * freq[None, :]
    table = jnp.concatenate([jnp.sin(angle), jnp.cos(angle)], axis=1)
    return jnp.concatenate(
        [jnp.take(table, row_pos, axis=0, mode="clip"), jnp.take(table, col_pos, axis=0, mode="clip")],
        axis=1,
    )


def key_labels(block_start, tok_rows, seg_ids, pad_mask):
    total = seg_ids.shape[0]
    index = block_start + jnp.arange(tok_rows, dtype=jnp.int32)
    inside = (index >= 0) & (index < total)
    clamped = jnp.clip(block_start, 0, total - tok_rows)
    seg_part = lax.dynamic_slice_in_dim(seg_ids, clamped, tok_rows)
    mask_part = lax.dynamic_slice_in_dim(pad_mask, clamped, tok_rows)
    return (jnp.where(inside, seg_part, -1), inside & (mask_part == 1))


def local(
    patches,
    image_sizes,
    seg_ids,
    pad_mask,
    ln1_gain,
    qkv_weight,
    out_weight,
    ln2_gain,
    fc1_weight,
    fc2_weight,
    proj_weight,
    owners,
):
    tok_rows, width = patches.shape
    seq_count = lax.axis_size("seq")
    tensor_count = lax.axis_size("tensor")
    seq_rank = lax.axis_index("seq")
    tensor_rank = lax.axis_index("tensor")
    first = seq_rank * tok_rows
    index = first + jnp.arange(tok_rows, dtype=jnp.int32)
    seg_local = lax.dynamic_slice_in_dim(seg_ids, first, tok_rows)
    valid_local = lax.dynamic_slice_in_dim(pad_mask, first, tok_rows).astype(jnp.float32)
    x0 = (
        patches.astype(jnp.float32)
        + position_table(seg_local, image_sizes, index, width) * valid_local[:, None]
    )
    h1 = layer_norm(x0, ln1_gain).astype(jnp.bfloat16)
    local_width = qkv_weight.shape[2]
    heads = local_width // HD
    qkv = jnp.dot(
        h1, qkv_weight.reshape(width, 3 * local_width), preferred_element_type=jnp.float32
    )
    qkv = qkv.astype(jnp.bfloat16).reshape(tok_rows, 3, local_width)
    queries = qkv[:, 0].reshape(tok_rows, heads, HD)
    pairs = qkv[:, 1:]
    reach = min((SIDE * SIDE + tok_rows - 2) // tok_rows, seq_count - 1)
    blocks = [pairs]
    block_starts = [first]
    for step in range(1, reach + 1):
        blocks.append(shifted(pairs, "seq", step))
        block_starts.append(first - step * tok_rows)
        blocks.append(shifted(pairs, "seq", -step))
        block_starts.append(first + step * tok_rows)
    labels = [key_labels(start, tok_rows, seg_ids, pad_mask) for start in block_starts]
    key_seg = jnp.concatenate([item[0] for item in labels])
    key_ok = jnp.concatenate([item[1] for item in labels])
    gathered_pairs = jnp.concatenate(blocks, axis=0)
    keys = gathered_pairs[:, 0].reshape(-1, heads, HD)
    values = gathered_pairs[:, 1].reshape(-1, heads, HD)
    allowed = ((seg_local[:, None] == key_seg[None, :]) & key_ok[None, :])[None, :, :]
    scores = jnp.einsum("qhe,khe->hqk", queries, keys, preferred_element_type=jnp.float32) * HD ** (
        -0.5
    )
    best = jnp.max(jnp.where(allowed, scores, -1e30), axis=2, keepdims=True)
    weights = jnp.where(allowed, jnp.exp(scores - best), 0.0)
    total = jnp.sum(weights, axis=2)
    mixed = jnp.einsum(
        "hqk,khe->qhe", weights.astype(jnp.bfloat16), values, preferred_element_type=jnp.float32
    )
    attended = (
        (mixed / jnp.maximum(total, 1.0).T[:, :, None])
        .astype(jnp.bfloat16)
        .reshape(tok_rows, local_width)
    )
    groups = tok_rows // 4
    rows = np.arange(tok_rows)
    quarter_order = jnp.asarray((rows % groups) * 4 + rows // groups, dtype=jnp.int32)

    def by_quarter(array):
        return jnp.take(array, quarter_order, axis=0, mode="clip")

    partial_attn = jnp.dot(by_quarter(attended), out_weight, preferred_element_type=jnp.float32)

    def pick_rows(array):
        return lax.dynamic_slice_in_dim(array, tensor_rank * groups, groups)

    valid_rows = pick_rows(by_quarter(valid_local)[:, None])
    attn_sum = tensor_reduce_scatter(partial_attn.reshape(tensor_count, -1, width))
    attn_full = tensor_all_gather(attn_sum.astype(jnp.bfloat16)).reshape(tok_rows, width)
    x1 = by_quarter(x0) + attn_full.astype(jnp.float32)
    h2 = layer_norm(x1, ln2_gain).astype(jnp.bfloat16)
    hidden = jax.nn.gelu(
        jnp.dot(h2, fc1_weight, preferred_element_type=jnp.float32), approximate=False
    ).astype(jnp.bfloat16)
    mlp_out = jnp.dot(hidden, fc2_weight, preferred_element_type=jnp.float32)
    mlp_part = tensor_reduce_scatter(mlp_out.reshape(tensor_count, groups, width))
    x1_rows = pick_rows(x1)
    own_quarter = ((x1_rows + mlp_part) * valid_rows).astype(jnp.bfloat16)
    gathered = lax.all_to_all(
        jnp.broadcast_to(own_quarter, (seq_count,) + own_quarter.shape),
        "seq",
        split_axis=0,
        concat_axis=0,
        tiled=True,
    ).reshape(seq_count * groups, width)
    partial_proj = jnp.dot(gathered, proj_weight, preferred_element_type=jnp.float32)
    quarter_rows = seq_count * groups // tensor_count
    proj_part = tensor_reduce_scatter(partial_proj.reshape(tensor_count, quarter_rows, -1))
    row_begin = tensor_rank * quarter_rows
    local_order = jnp.arange(quarter_rows, dtype=jnp.int32)
    merged_seg = jnp.take(seg_ids.reshape(-1, 4)[:, 0], row_begin + local_order, mode="clip")
    merged_valid = jnp.take(pad_mask.reshape(-1, 4)[:, 0], row_begin + local_order, mode="clip")
    image_ids = jnp.arange(image_sizes.shape[0], dtype=jnp.int32)
    member = ((merged_seg[:, None] == image_ids[None, :]) & (merged_valid[:, None] == 1)).astype(
        jnp.float32
    )
    row_squares = jnp.sum(proj_part * proj_part, axis=1)
    row_peak = jnp.max(jnp.abs(proj_part), axis=1)
    local_sums = jnp.dot(row_squares, member, precision=lax.Precision.HIGHEST)
    local_peaks = jnp.max(jnp.where(member > 0, row_peak[:, None], 0.0), axis=0)
    emb = proj_part.astype(jnp.bfloat16)
    capacity = 2 * quarter_rows // seq_count
    owner_rows = lax.dynamic_slice_in_dim(owners[:, 0], row_begin, quarter_rows)
    onehot = (owner_rows[:, None] == jnp.arange(seq_count, dtype=jnp.int32)[None, :]).astype(
        jnp.int32
    )
    rank = jnp.cumsum(onehot, axis=0) - onehot
    slot = jnp.sum(onehot * rank, axis=1)
    target = jnp.take(owner_rows * capacity + slot, local_order, mode="clip")
    place = (jnp.arange(seq_count * capacity, dtype=jnp.int32)[:, None] == target[None, :]).astype(
        jnp.bfloat16
    )
    buffer = jnp.dot(place, emb, preferred_element_type=jnp.float32).astype(jnp.bfloat16)
    buffer = buffer.reshape(seq_count, capacity, emb.shape[1])
    stats = jnp.stack([local_sums, local_peaks]).reshape(-1)
    high = stats.astype(jnp.bfloat16)
    low = (stats - high.astype(jnp.float32)).astype(jnp.bfloat16)
    extra = jnp.zeros((8, emb.shape[1]), jnp.bfloat16)
    extra = extra.at[0, : stats.shape[0]].set(high).at[1, : stats.shape[0]].set(low)
    buffer = jnp.concatenate([buffer, jnp.broadcast_to(extra, (seq_count,) + extra.shape)], axis=1)
    arrived = lax.all_to_all(buffer, "seq", split_axis=0, concat_axis=2, tiled=True)
    delivered = arrived[:, :capacity].reshape(1, 1, capacity, arrived.shape[2])
    parts = arrived[0, capacity : capacity + 2].reshape(2, seq_count, emb.shape[1])
    parts = parts[:, :, : stats.shape[0]].astype(jnp.float32)
    parts = (parts[0] + parts[1]).reshape(seq_count, 2, -1)
    stats = jnp.stack([jnp.sum(parts[:, 0], axis=0), jnp.max(parts[:, 1], axis=0)])
    for bit in (1, 2):
        if bit < tensor_count:
            other = swap(stats, "tensor", bit)
            stats = jnp.stack([stats[0] + other[0], jnp.maximum(stats[1], other[1])])
    sums, image_peak = stats[0], stats[1]
    counts = (image_sizes[:, 0] * image_sizes[:, 1] // 4).astype(jnp.float32)
    image_rms = jnp.sqrt(sums / (PROJ * jnp.maximum(counts, 1.0)))
    return (delivered, image_rms, image_peak)


def solution(mesh):
    in_specs = (
        P(("dp", "seq"), None),
        P("dp", None),
        P("dp"),
        P("dp"),
        P(),
        P(None, None, "tensor"),
        P("tensor", None),
        P(),
        P(None, "tensor"),
        P("tensor", None),
        P("tensor", "seq"),
        P("dp", None),
    )
    out_specs = (P(("dp", "seq"), "tensor", None, None), P("dp"), P("dp"))
    return jax.shard_map(local, mesh=mesh, in_specs=in_specs, out_specs=out_specs, check_vma=False)
```

```python
import math

import jax
import numpy as np
import jax.numpy as jnp
from jax import lax
from jax.sharding import PartitionSpec as P

HD = 104
PROJ = 4096
SIDE = 32


EPS = 1e-06


def shifted(value, axis, steps):
    count = lax.axis_size(axis)
    leading, last = (max(0, -steps), min(count, count - steps))
    return lax.ppermute(value, axis, [(source, source + steps) for source in range(leading, last)])


def swap(value, axis, bit):
    count = lax.axis_size(axis)
    return lax.ppermute(value, axis, [(source, source ^ bit) for source in range(count)])


def take_half(value, index, axis):
    return lax.dynamic_index_in_dim(value, index, axis, keepdims=False)


def tensor_reduce_scatter(parts, rank=None):
    if rank is None:
        rank = lax.axis_index("tensor")
    low, high = rank % 2, rank // 2
    quads = parts.reshape((2, 2) + parts.shape[1:])
    kept = take_half(quads, low, 1)
    sent = take_half(quads, 1 - low, 1).astype(jnp.bfloat16)
    halves = kept + swap(sent, "tensor", 1).astype(jnp.float32)
    sent = take_half(halves, 1 - high, 0).astype(jnp.bfloat16)
    return take_half(halves, high, 0) + swap(sent, "tensor", 2).astype(jnp.float32)


def tensor_all_reduce(parts):
    rank = lax.axis_index("tensor")
    low = rank % 2
    quads = parts.reshape((2, 2) + parts.shape[1:])
    sent = take_half(quads, 1 - low, 1).astype(jnp.bfloat16)
    halves = (take_half(quads, low, 1) + swap(sent, "tensor", 1).astype(jnp.float32)).astype(jnp.bfloat16)
    total = (halves.astype(jnp.float32) + swap(halves, "tensor", 2).astype(jnp.float32)).astype(jnp.bfloat16)
    other = swap(total, "tensor", 1)
    return jnp.where(low == 0, jnp.stack([total, other], 1), jnp.stack([other, total], 1))


def tensor_all_gather(mine):
    rank = lax.axis_index("tensor")
    low, high = rank % 2, rank // 2
    other = swap(mine, "tensor", 2)
    pair = jnp.where(high == 0, jnp.stack([mine, other]), jnp.stack([other, mine]))
    other = swap(pair, "tensor", 1)
    return jnp.where(low == 0, jnp.stack([pair, other], 1), jnp.stack([other, pair], 1))


def butterfly_stats(stats):
    for axis, bits in (("tensor", (1, 2)), ("seq", (1, 2, 4))):
        for bit in bits:
            if bit < lax.axis_size(axis):
                other = swap(stats, axis, bit)
                stats = jnp.stack([stats[0] + other[0], jnp.maximum(stats[1], other[1])])
    return stats


def layer_norm(values, gain):
    mean = jnp.mean(values, axis=-1, keepdims=True)
    centred = values - mean
    spread = jnp.mean(centred * centred, axis=-1, keepdims=True)
    return centred * lax.rsqrt(spread + EPS) * gain


def position_table(seg_local, image_sizes, index, width):
    heights = image_sizes[:, 0]
    widths = image_sizes[:, 1]
    areas = heights * widths
    starts = jnp.cumsum(areas) - areas
    image_ids = jnp.arange(image_sizes.shape[0], dtype=jnp.int32)
    member = (seg_local[:, None] == image_ids[None, :]).astype(jnp.int32)
    begin = jnp.sum(member * starts[None, :], axis=1)
    across = jnp.sum(member * widths[None, :], axis=1)
    offset = index - begin
    blocks = offset // 4
    inner = offset % 4
    half = jnp.maximum(across // 2, 1)
    row_pos = jnp.clip(2 * (blocks // half) + inner // 2, 0, SIDE - 1)
    col_pos = jnp.clip(2 * (blocks % half) + inner % 2, 0, SIDE - 1)
    quarter = width // 4
    freq = jnp.exp(jnp.arange(quarter, dtype=jnp.float32) * (-math.log(10000.0) / quarter))
    angle = jnp.arange(SIDE, dtype=jnp.float32)[:, None] * freq[None, :]
    table = jnp.concatenate([jnp.sin(angle), jnp.cos(angle)], axis=1)
    return jnp.concatenate(
        [jnp.take(table, row_pos, axis=0, mode="clip"), jnp.take(table, col_pos, axis=0, mode="clip")],
        axis=1,
    )


def key_labels(block_start, tok_rows, seg_ids, pad_mask):
    total = seg_ids.shape[0]
    index = block_start + jnp.arange(tok_rows, dtype=jnp.int32)
    inside = (index >= 0) & (index < total)
    clamped = jnp.clip(block_start, 0, total - tok_rows)
    seg_part = lax.dynamic_slice_in_dim(seg_ids, clamped, tok_rows)
    mask_part = lax.dynamic_slice_in_dim(pad_mask, clamped, tok_rows)
    return (jnp.where(inside, seg_part, -1), inside & (mask_part == 1))


def local(
    patches,
    image_sizes,
    seg_ids,
    pad_mask,
    ln1_gain,
    qkv_weight,
    out_weight,
    ln2_gain,
    fc1_weight,
    fc2_weight,
    proj_weight,
    owners,
):
    tok_rows, width = patches.shape
    seq_count = lax.axis_size("seq")
    tensor_count = lax.axis_size("tensor")
    seq_rank = lax.axis_index("seq")
    tensor_rank = lax.axis_index("tensor")
    first = seq_rank * tok_rows
    index = first + jnp.arange(tok_rows, dtype=jnp.int32)
    seg_local = lax.dynamic_slice_in_dim(seg_ids, first, tok_rows)
    valid_local = lax.dynamic_slice_in_dim(pad_mask, first, tok_rows).astype(jnp.float32)
    x0 = (
        patches.astype(jnp.float32)
        + position_table(seg_local, image_sizes, index, width) * valid_local[:, None]
    )
    h1 = layer_norm(x0, ln1_gain).astype(jnp.bfloat16)
    local_width = qkv_weight.shape[2]
    heads = local_width // HD
    qkv = jnp.dot(
        h1, qkv_weight.reshape(width, 3 * local_width), preferred_element_type=jnp.float32
    )
    qkv = qkv.astype(jnp.bfloat16).reshape(tok_rows, 3, local_width)
    queries = qkv[:, 0].reshape(tok_rows, heads, HD)
    pairs = qkv[:, 1:]
    reach = min((SIDE * SIDE + tok_rows - 2) // tok_rows, seq_count - 1)
    blocks = [pairs]
    block_starts = [first]
    for step in range(1, reach + 1):
        blocks.append(shifted(pairs, "seq", step))
        block_starts.append(first - step * tok_rows)
        blocks.append(shifted(pairs, "seq", -step))
        block_starts.append(first + step * tok_rows)
    labels = [key_labels(start, tok_rows, seg_ids, pad_mask) for start in block_starts]
    key_seg = jnp.concatenate([item[0] for item in labels])
    key_ok = jnp.concatenate([item[1] for item in labels])
    gathered_pairs = jnp.concatenate(blocks, axis=0)
    keys = gathered_pairs[:, 0].reshape(-1, heads, HD)
    values = gathered_pairs[:, 1].reshape(-1, heads, HD)
    allowed = ((seg_local[:, None] == key_seg[None, :]) & key_ok[None, :])[None, :, :]
    scores = jnp.einsum("qhe,khe->hqk", queries, keys, preferred_element_type=jnp.float32) * HD ** (
        -0.5
    )
    best = jnp.max(jnp.where(allowed, scores, -1e30), axis=2, keepdims=True)
    weights = jnp.where(allowed, jnp.exp(scores - best), 0.0)
    total = jnp.sum(weights, axis=2)
    mixed = jnp.einsum(
        "hqk,khe->qhe", weights.astype(jnp.bfloat16), values, preferred_element_type=jnp.float32
    )
    attended = (
        (mixed / jnp.maximum(total, 1.0).T[:, :, None])
        .astype(jnp.bfloat16)
        .reshape(tok_rows, local_width)
    )
    groups = tok_rows // 4
    rows = np.arange(tok_rows)
    quarter_order = jnp.asarray((rows % groups) * 4 + rows // groups, dtype=jnp.int32)

    def by_quarter(array):
        return jnp.take(array, quarter_order, axis=0, mode="clip")

    partial_attn = jnp.dot(by_quarter(attended), out_weight, preferred_element_type=jnp.float32)

    def pick_rows(array):
        return lax.dynamic_slice_in_dim(array, tensor_rank * groups, groups)

    valid_rows = pick_rows(by_quarter(valid_local)[:, None])
    attn_full = tensor_all_reduce(partial_attn.reshape(tensor_count, -1, width)).reshape(tok_rows, width)
    x1 = by_quarter(x0) + attn_full.astype(jnp.float32)
    h2 = layer_norm(x1, ln2_gain).astype(jnp.bfloat16)
    hidden = jax.nn.gelu(
        jnp.dot(h2, fc1_weight, preferred_element_type=jnp.float32), approximate=False
    ).astype(jnp.bfloat16)
    mlp_out = jnp.dot(hidden, fc2_weight, preferred_element_type=jnp.float32)
    mlp_part = tensor_reduce_scatter(mlp_out.reshape(tensor_count, groups, width))
    x1_rows = pick_rows(x1)
    own_quarter = ((x1_rows + mlp_part) * valid_rows).astype(jnp.bfloat16)
    gathered = lax.all_to_all(
        jnp.broadcast_to(own_quarter, (seq_count,) + own_quarter.shape),
        "seq",
        split_axis=0,
        concat_axis=0,
        tiled=True,
    ).reshape(seq_count * groups, width)
    partial_proj = jnp.dot(gathered, proj_weight, preferred_element_type=jnp.float32)
    quarter_rows = seq_count * groups // tensor_count
    proj_part = tensor_reduce_scatter(partial_proj.reshape(tensor_count, quarter_rows, -1))
    row_begin = tensor_rank * quarter_rows
    merged_seg = lax.dynamic_slice_in_dim(seg_ids.reshape(-1, 4)[:, 0], row_begin, quarter_rows)
    merged_valid = lax.dynamic_slice_in_dim(pad_mask.reshape(-1, 4)[:, 0], row_begin, quarter_rows)
    image_ids = jnp.arange(image_sizes.shape[0], dtype=jnp.int32)
    member = ((merged_seg[:, None] == image_ids[None, :]) & (merged_valid[:, None] == 1)).astype(
        jnp.float32
    )
    row_squares = jnp.sum(proj_part * proj_part, axis=1)
    row_peak = jnp.max(jnp.abs(proj_part), axis=1)
    local_sums = jnp.dot(row_squares, member, precision=lax.Precision.HIGHEST)
    local_peaks = jnp.max(jnp.where(member > 0, row_peak[:, None], 0.0), axis=0)
    emb = proj_part.astype(jnp.bfloat16)
    capacity = 2 * quarter_rows // seq_count
    owner_rows = lax.dynamic_slice_in_dim(owners[:, 0], row_begin, quarter_rows)
    onehot = (owner_rows[:, None] == jnp.arange(seq_count, dtype=jnp.int32)[None, :]).astype(
        jnp.int32
    )
    rank = jnp.cumsum(onehot, axis=0) - onehot
    slot = jnp.sum(onehot * rank, axis=1)
    target = owner_rows * capacity + slot
    place = (jnp.arange(seq_count * capacity, dtype=jnp.int32)[:, None] == target[None, :]).astype(
        jnp.bfloat16
    )
    buffer = jnp.dot(place, emb, preferred_element_type=jnp.float32).astype(jnp.bfloat16)
    buffer = buffer.reshape(seq_count, capacity, emb.shape[1])
    stats = jnp.stack([local_sums, local_peaks]).reshape(-1)
    high = stats.astype(jnp.bfloat16)
    low = (stats - high.astype(jnp.float32)).astype(jnp.bfloat16)
    extra = jnp.zeros((8, emb.shape[1]), jnp.bfloat16)
    extra = extra.at[0, : stats.shape[0]].set(high).at[1, : stats.shape[0]].set(low)
    buffer = jnp.concatenate([buffer, jnp.broadcast_to(extra, (seq_count,) + extra.shape)], axis=1)
    arrived = lax.all_to_all(buffer, "seq", split_axis=0, concat_axis=2, tiled=True)
    delivered = arrived[:, :capacity].reshape(1, 1, capacity, arrived.shape[2])
    parts = arrived[0, capacity : capacity + 2].reshape(2, seq_count, emb.shape[1])
    parts = parts[:, :, : stats.shape[0]].astype(jnp.float32)
    parts = (parts[0] + parts[1]).reshape(seq_count, 2, -1)
    stats = jnp.stack([jnp.sum(parts[:, 0], axis=0), jnp.max(parts[:, 1], axis=0)])
    for bit in (1, 2):
        if bit < tensor_count:
            other = swap(stats, "tensor", bit)
            stats = jnp.stack([stats[0] + other[0], jnp.maximum(stats[1], other[1])])
    sums, image_peak = stats[0], stats[1]
    counts = (image_sizes[:, 0] * image_sizes[:, 1] // 4).astype(jnp.float32)
    image_rms = jnp.sqrt(sums / (PROJ * jnp.maximum(counts, 1.0)))
    return (delivered, image_rms, image_peak)


def solution(mesh):
    in_specs = (
        P(("dp", "seq"), None),
        P("dp", None),
        P("dp"),
        P("dp"),
        P(),
        P(None, None, "tensor"),
        P("tensor", None),
        P(),
        P(None, "tensor"),
        P("tensor", None),
        P("tensor", "seq"),
        P("dp", None),
    )
    out_specs = (P(("dp", "seq"), "tensor", None, None), P("dp"), P("dp"))
    return jax.shard_map(local, mesh=mesh, in_specs=in_specs, out_specs=out_specs, check_vma=False)
```

```python
import math

import jax
import numpy as np
import jax.numpy as jnp
from jax import lax
from jax.sharding import PartitionSpec as P

HD = 104
PROJ = 4096
SIDE = 32


EPS = 1e-06


def shifted(value, axis, steps):
    count = lax.axis_size(axis)
    leading, last = (max(0, -steps), min(count, count - steps))
    return lax.ppermute(value, axis, [(source, source + steps) for source in range(leading, last)])


def swap(value, axis, bit):
    count = lax.axis_size(axis)
    return lax.ppermute(value, axis, [(source, source ^ bit) for source in range(count)])


def take_half(value, index, axis):
    return lax.dynamic_index_in_dim(value, index, axis, keepdims=False)


def tensor_reduce_scatter(parts, rank=None):
    if rank is None:
        rank = lax.axis_index("tensor")
    low, high = rank % 2, rank // 2
    quads = parts.reshape((2, 2) + parts.shape[1:])
    kept = take_half(quads, low, 1)
    sent = take_half(quads, 1 - low, 1).astype(jnp.bfloat16)
    halves = kept + swap(sent, "tensor", 1).astype(jnp.float32)
    sent = take_half(halves, 1 - high, 0).astype(jnp.bfloat16)
    return take_half(halves, high, 0) + swap(sent, "tensor", 2).astype(jnp.float32)


def tensor_all_reduce_begin(parts):
    low = lax.axis_index("tensor") % 2
    quads = parts.reshape((2, 2) + parts.shape[1:])
    sent = take_half(quads, 1 - low, 1).astype(jnp.bfloat16)
    return (take_half(quads, low, 1) + swap(sent, "tensor", 1).astype(jnp.float32)).astype(jnp.bfloat16)


def tensor_all_reduce_finish(halves):
    low = lax.axis_index("tensor") % 2
    other = swap(halves, "tensor", 2)
    total = (halves.astype(jnp.float32) + other.astype(jnp.float32)).astype(jnp.bfloat16)
    other = swap(total, "tensor", 1)
    return jnp.where(low == 0, jnp.stack([total, other], 1), jnp.stack([other, total], 1))


def layer_norm(values, gain):
    mean = jnp.mean(values, axis=-1, keepdims=True)
    centred = values - mean
    spread = jnp.mean(centred * centred, axis=-1, keepdims=True)
    return centred * lax.rsqrt(spread + EPS) * gain


def position_table(seg_local, image_sizes, index, width):
    heights = image_sizes[:, 0]
    widths = image_sizes[:, 1]
    areas = heights * widths
    starts = jnp.cumsum(areas) - areas
    image_ids = jnp.arange(image_sizes.shape[0], dtype=jnp.int32)
    member = (seg_local[:, None] == image_ids[None, :]).astype(jnp.int32)
    begin = jnp.sum(member * starts[None, :], axis=1)
    across = jnp.sum(member * widths[None, :], axis=1)
    offset = index - begin
    blocks = offset // 4
    inner = offset % 4
    half = jnp.maximum(across // 2, 1)
    row_pos = jnp.clip(2 * (blocks // half) + inner // 2, 0, SIDE - 1)
    col_pos = jnp.clip(2 * (blocks % half) + inner % 2, 0, SIDE - 1)
    quarter = width // 4
    freq = jnp.exp(jnp.arange(quarter, dtype=jnp.float32) * (-math.log(10000.0) / quarter))
    angle = jnp.arange(SIDE, dtype=jnp.float32)[:, None] * freq[None, :]
    table = jnp.concatenate([jnp.sin(angle), jnp.cos(angle)], axis=1)
    return jnp.concatenate(
        [jnp.take(table, row_pos, axis=0, mode="clip"), jnp.take(table, col_pos, axis=0, mode="clip")],
        axis=1,
    )


def key_labels(block_start, tok_rows, seg_ids, pad_mask):
    total = seg_ids.shape[0]
    index = block_start + jnp.arange(tok_rows, dtype=jnp.int32)
    inside = (index >= 0) & (index < total)
    clamped = jnp.clip(block_start, 0, total - tok_rows)
    seg_part = lax.dynamic_slice_in_dim(seg_ids, clamped, tok_rows)
    mask_part = lax.dynamic_slice_in_dim(pad_mask, clamped, tok_rows)
    return (jnp.where(inside, seg_part, -1), inside & (mask_part == 1))


def local(
    patches,
    image_sizes,
    seg_ids,
    pad_mask,
    ln1_gain,
    qkv_weight,
    out_weight,
    ln2_gain,
    fc1_weight,
    fc2_weight,
    proj_weight,
    owners,
):
    tok_rows, width = patches.shape
    seq_count = lax.axis_size("seq")
    tensor_count = lax.axis_size("tensor")
    seq_rank = lax.axis_index("seq")
    tensor_rank = lax.axis_index("tensor")
    first = seq_rank * tok_rows
    index = first + jnp.arange(tok_rows, dtype=jnp.int32)
    seg_local = lax.dynamic_slice_in_dim(seg_ids, first, tok_rows)
    valid_local = lax.dynamic_slice_in_dim(pad_mask, first, tok_rows).astype(jnp.float32)
    x0 = (
        patches.astype(jnp.float32)
        + position_table(seg_local, image_sizes, index, width) * valid_local[:, None]
    )
    h1 = layer_norm(x0, ln1_gain).astype(jnp.bfloat16)
    local_width = qkv_weight.shape[2]
    heads = local_width // HD
    qkv = jnp.dot(
        h1, qkv_weight.reshape(width, 3 * local_width), preferred_element_type=jnp.float32
    )
    qkv = qkv.astype(jnp.bfloat16).reshape(tok_rows, 3, local_width)
    queries = qkv[:, 0].reshape(tok_rows, heads, HD)
    pairs = qkv[:, 1:]
    reach = min((SIDE * SIDE + tok_rows - 2) // tok_rows, seq_count - 1)
    blocks = [pairs]
    block_starts = [first]
    for step in range(1, reach + 1):
        blocks.append(shifted(pairs, "seq", step))
        block_starts.append(first - step * tok_rows)
        blocks.append(shifted(pairs, "seq", -step))
        block_starts.append(first + step * tok_rows)
    labels = [key_labels(start, tok_rows, seg_ids, pad_mask) for start in block_starts]
    key_seg = jnp.concatenate([item[0] for item in labels])
    key_ok = jnp.concatenate([item[1] for item in labels])
    gathered_pairs = jnp.concatenate(blocks, axis=0)
    keys = gathered_pairs[:, 0].reshape(-1, heads, HD)
    values = gathered_pairs[:, 1].reshape(-1, heads, HD)
    groups = tok_rows // 4
    rows = np.arange(tok_rows)
    quarter_order = jnp.asarray((rows % groups) * 4 + rows // groups, dtype=jnp.int32)

    def by_quarter(array):
        return jnp.take(array, quarter_order, axis=0, mode="clip")

    def attend(query_rows, query_seg):
        allowed = ((query_seg[:, None] == key_seg[None, :]) & key_ok[None, :])[None, :, :]
        scores = jnp.einsum("qhe,khe->hqk", query_rows, keys, preferred_element_type=jnp.float32)
        scores = scores * HD ** (-0.5)
        best = jnp.max(jnp.where(allowed, scores, -1e30), axis=2, keepdims=True)
        weights = jnp.where(allowed, jnp.exp(scores - best), 0.0)
        total = jnp.sum(weights, axis=2)
        mixed = jnp.einsum(
            "hqk,khe->qhe", weights.astype(jnp.bfloat16), values, preferred_element_type=jnp.float32
        )
        attended = (
            (mixed / jnp.maximum(total, 1.0).T[:, :, None])
            .astype(jnp.bfloat16)
            .reshape(query_rows.shape[0], local_width)
        )
        partial = jnp.dot(attended, out_weight, preferred_element_type=jnp.float32)
        return tensor_all_reduce_begin(partial.reshape(tensor_count, -1, width))

    ordered_queries = by_quarter(queries)
    ordered_seg = by_quarter(seg_local)
    half = tok_rows // 2
    first_half = attend(ordered_queries[:half], ordered_seg[:half])
    first_half, later_queries = lax.optimization_barrier((first_half, ordered_queries[half:]))
    first_half = tensor_all_reduce_finish(first_half).reshape(-1, width)
    second_half = attend(later_queries, ordered_seg[half:])
    second_half = tensor_all_reduce_finish(second_half).reshape(-1, width)
    attn_full = jnp.concatenate([first_half, second_half])

    def pick_rows(array):
        return lax.dynamic_slice_in_dim(array, tensor_rank * groups, groups)

    valid_rows = pick_rows(by_quarter(valid_local)[:, None])
    x1 = by_quarter(x0) + attn_full.astype(jnp.float32)
    h2 = layer_norm(x1, ln2_gain).astype(jnp.bfloat16)
    hidden = jax.nn.gelu(
        jnp.dot(h2, fc1_weight, preferred_element_type=jnp.float32), approximate=False
    ).astype(jnp.bfloat16)
    mlp_out = jnp.dot(hidden, fc2_weight, preferred_element_type=jnp.float32)
    mlp_part = tensor_reduce_scatter(mlp_out.reshape(tensor_count, groups, width))
    x1_rows = pick_rows(x1)
    own_quarter = ((x1_rows + mlp_part) * valid_rows).astype(jnp.bfloat16)
    gathered = lax.all_to_all(
        jnp.broadcast_to(own_quarter, (seq_count,) + own_quarter.shape),
        "seq",
        split_axis=0,
        concat_axis=0,
        tiled=True,
    ).reshape(seq_count * groups, width)
    partial_proj = jnp.dot(gathered, proj_weight, preferred_element_type=jnp.float32)
    quarter_rows = seq_count * groups // tensor_count
    proj_part = tensor_reduce_scatter(partial_proj.reshape(tensor_count, quarter_rows, -1))
    row_begin = tensor_rank * quarter_rows
    merged_seg = lax.dynamic_slice_in_dim(seg_ids.reshape(-1, 4)[:, 0], row_begin, quarter_rows)
    merged_valid = lax.dynamic_slice_in_dim(pad_mask.reshape(-1, 4)[:, 0], row_begin, quarter_rows)
    image_ids = jnp.arange(image_sizes.shape[0], dtype=jnp.int32)
    member = ((merged_seg[:, None] == image_ids[None, :]) & (merged_valid[:, None] == 1)).astype(
        jnp.float32
    )
    row_squares = jnp.sum(proj_part * proj_part, axis=1)
    row_peak = jnp.max(jnp.abs(proj_part), axis=1)
    local_sums = jnp.dot(row_squares, member, precision=lax.Precision.HIGHEST)
    local_peaks = jnp.max(jnp.where(member > 0, row_peak[:, None], 0.0), axis=0)
    emb = proj_part.astype(jnp.bfloat16)
    capacity = 2 * quarter_rows // seq_count
    owner_rows = lax.dynamic_slice_in_dim(owners[:, 0], row_begin, quarter_rows)
    onehot = (owner_rows[:, None] == jnp.arange(seq_count, dtype=jnp.int32)[None, :]).astype(
        jnp.int32
    )
    rank = jnp.cumsum(onehot, axis=0) - onehot
    slot = jnp.sum(onehot * rank, axis=1)
    target = owner_rows * capacity + slot
    place = (jnp.arange(seq_count * capacity, dtype=jnp.int32)[:, None] == target[None, :]).astype(
        jnp.bfloat16
    )
    buffer = jnp.dot(place, emb, preferred_element_type=jnp.float32).astype(jnp.bfloat16)
    buffer = buffer.reshape(seq_count, capacity, emb.shape[1])
    stats = jnp.stack([local_sums, local_peaks]).reshape(-1)
    high = stats.astype(jnp.bfloat16)
    low = (stats - high.astype(jnp.float32)).astype(jnp.bfloat16)
    extra = jnp.zeros((8, emb.shape[1]), jnp.bfloat16)
    extra = extra.at[0, : stats.shape[0]].set(high).at[1, : stats.shape[0]].set(low)
    buffer = jnp.concatenate([buffer, jnp.broadcast_to(extra, (seq_count,) + extra.shape)], axis=1)
    arrived = lax.all_to_all(buffer, "seq", split_axis=0, concat_axis=2, tiled=True)
    delivered = arrived[:, :capacity].reshape(1, 1, capacity, arrived.shape[2])
    parts = arrived[0, capacity : capacity + 2].reshape(2, seq_count, emb.shape[1])
    parts = parts[:, :, : stats.shape[0]].astype(jnp.float32)
    parts = (parts[0] + parts[1]).reshape(seq_count, 2, -1)
    stats = jnp.stack([jnp.sum(parts[:, 0], axis=0), jnp.max(parts[:, 1], axis=0)])
    for bit in (1, 2):
        if bit < tensor_count:
            other = swap(stats, "tensor", bit)
            stats = jnp.stack([stats[0] + other[0], jnp.maximum(stats[1], other[1])])
    sums, image_peak = stats[0], stats[1]
    counts = (image_sizes[:, 0] * image_sizes[:, 1] // 4).astype(jnp.float32)
    image_rms = jnp.sqrt(sums / (PROJ * jnp.maximum(counts, 1.0)))
    return (delivered, image_rms, image_peak)


def solution(mesh):
    in_specs = (
        P(("dp", "seq"), None),
        P("dp", None),
        P("dp"),
        P("dp"),
        P(),
        P(None, None, "tensor"),
        P("tensor", None),
        P(),
        P(None, "tensor"),
        P("tensor", None),
        P("tensor", "seq"),
        P("dp", None),
    )
    out_specs = (P(("dp", "seq"), "tensor", None, None), P("dp"), P("dp"))

    return jax.shard_map(local, mesh=mesh, in_specs=in_specs, out_specs=out_specs, check_vma=False)
```

```python
import math

import jax
import numpy as np
import jax.numpy as jnp
from jax import lax
from jax.sharding import PartitionSpec as P

HD = 104
PROJ = 4096
SIDE = 32


EPS = 1e-06


def shifted(value, axis, steps):
    count = lax.axis_size(axis)
    leading, last = (max(0, -steps), min(count, count - steps))
    return lax.ppermute(value, axis, [(source, source + steps) for source in range(leading, last)])


def swap(value, axis, bit):
    count = lax.axis_size(axis)
    return lax.ppermute(value, axis, [(source, source ^ bit) for source in range(count)])


def take_half(value, index, axis):
    return lax.dynamic_index_in_dim(value, index, axis, keepdims=False)


def tensor_reduce_scatter(parts, rank=None):
    if rank is None:
        rank = lax.axis_index("tensor")
    low, high = rank % 2, rank // 2
    quads = parts.reshape((2, 2) + parts.shape[1:])
    kept = take_half(quads, low, 1)
    sent = take_half(quads, 1 - low, 1).astype(jnp.bfloat16)
    halves = kept + swap(sent, "tensor", 1).astype(jnp.float32)
    sent = take_half(halves, 1 - high, 0).astype(jnp.bfloat16)
    return take_half(halves, high, 0) + swap(sent, "tensor", 2).astype(jnp.float32)


def tensor_all_reduce(parts):
    rank = lax.axis_index("tensor")
    low = rank % 2
    quads = parts.reshape((2, 2) + parts.shape[1:])
    sent = take_half(quads, 1 - low, 1).astype(jnp.bfloat16)
    halves = (take_half(quads, low, 1) + swap(sent, "tensor", 1).astype(jnp.float32)).astype(jnp.bfloat16)
    total = (halves.astype(jnp.float32) + swap(halves, "tensor", 2).astype(jnp.float32)).astype(jnp.bfloat16)
    other = swap(total, "tensor", 1)
    return jnp.where(low == 0, jnp.stack([total, other], 1), jnp.stack([other, total], 1))


def layer_norm(values, gain):
    mean = jnp.mean(values, axis=-1, keepdims=True)
    centred = values - mean
    spread = jnp.mean(centred * centred, axis=-1, keepdims=True)
    return centred * lax.rsqrt(spread + EPS) * gain


def position_table(seg_local, image_sizes, index, width):
    heights = image_sizes[:, 0]
    widths = image_sizes[:, 1]
    areas = heights * widths
    starts = jnp.cumsum(areas) - areas
    image_ids = jnp.arange(image_sizes.shape[0], dtype=jnp.int32)
    member = (seg_local[:, None] == image_ids[None, :]).astype(jnp.int32)
    begin = jnp.sum(member * starts[None, :], axis=1)
    across = jnp.sum(member * widths[None, :], axis=1)
    offset = index - begin
    blocks = offset // 4
    inner = offset % 4
    half = jnp.maximum(across // 2, 1)
    row_pos = jnp.clip(2 * (blocks // half) + inner // 2, 0, SIDE - 1)
    col_pos = jnp.clip(2 * (blocks % half) + inner % 2, 0, SIDE - 1)
    quarter = width // 4
    freq = jnp.exp(jnp.arange(quarter, dtype=jnp.float32) * (-math.log(10000.0) / quarter))
    angle = jnp.arange(SIDE, dtype=jnp.float32)[:, None] * freq[None, :]
    table = jnp.concatenate([jnp.sin(angle), jnp.cos(angle)], axis=1)
    return jnp.concatenate(
        [jnp.take(table, row_pos, axis=0, mode="clip"), jnp.take(table, col_pos, axis=0, mode="clip")],
        axis=1,
    )


def key_labels(block_start, tok_rows, seg_ids, pad_mask):
    total = seg_ids.shape[0]
    index = block_start + jnp.arange(tok_rows, dtype=jnp.int32)
    inside = (index >= 0) & (index < total)
    clamped = jnp.clip(block_start, 0, total - tok_rows)
    seg_part = lax.dynamic_slice_in_dim(seg_ids, clamped, tok_rows)
    mask_part = lax.dynamic_slice_in_dim(pad_mask, clamped, tok_rows)
    return (jnp.where(inside, seg_part, -1), inside & (mask_part == 1))


def local(
    patches,
    image_sizes,
    seg_ids,
    pad_mask,
    ln1_gain,
    qkv_weight,
    out_weight,
    ln2_gain,
    fc1_weight,
    fc2_weight,
    proj_weight,
    owners,
):
    tok_rows, width = patches.shape
    seq_count = lax.axis_size("seq")
    tensor_count = lax.axis_size("tensor")
    seq_rank = lax.axis_index("seq")
    tensor_rank = lax.axis_index("tensor")
    first = seq_rank * tok_rows
    index = first + jnp.arange(tok_rows, dtype=jnp.int32)
    seg_local = lax.dynamic_slice_in_dim(seg_ids, first, tok_rows)
    valid_local = lax.dynamic_slice_in_dim(pad_mask, first, tok_rows).astype(jnp.float32)
    x0 = (
        patches.astype(jnp.float32)
        + position_table(seg_local, image_sizes, index, width) * valid_local[:, None]
    )
    h1 = layer_norm(x0, ln1_gain).astype(jnp.bfloat16)
    local_width = qkv_weight.shape[2]
    heads = local_width // HD
    qkv = jnp.dot(
        h1, qkv_weight.reshape(width, 3 * local_width), preferred_element_type=jnp.float32
    )
    qkv = qkv.astype(jnp.bfloat16).reshape(tok_rows, 3, local_width)
    queries = qkv[:, 0].reshape(tok_rows, heads, HD)
    pairs = qkv[:, 1:]
    reach = min((SIDE * SIDE + tok_rows - 2) // tok_rows, seq_count - 1)
    blocks = [pairs]
    block_starts = [first]
    for step in range(1, reach + 1):
        blocks.append(shifted(pairs, "seq", step))
        block_starts.append(first - step * tok_rows)
        blocks.append(shifted(pairs, "seq", -step))
        block_starts.append(first + step * tok_rows)
    labels = [key_labels(start, tok_rows, seg_ids, pad_mask) for start in block_starts]
    key_seg = jnp.concatenate([item[0] for item in labels])
    key_ok = jnp.concatenate([item[1] for item in labels])
    gathered_pairs = jnp.concatenate(blocks, axis=0)
    keys = gathered_pairs[:, 0].reshape(-1, heads, HD)
    values = gathered_pairs[:, 1].reshape(-1, heads, HD)
    allowed = ((seg_local[:, None] == key_seg[None, :]) & key_ok[None, :])[None, :, :]
    scores = jnp.einsum("qhe,khe->hqk", queries, keys, preferred_element_type=jnp.float32) * HD ** (
        -0.5
    )
    best = jnp.max(jnp.where(allowed, scores, -1e30), axis=2, keepdims=True)
    weights = jnp.where(allowed, jnp.exp(scores - best), 0.0)
    total = jnp.sum(weights, axis=2)
    mixed = jnp.einsum(
        "hqk,khe->qhe", weights.astype(jnp.bfloat16), values, preferred_element_type=jnp.float32
    )
    attended = (
        (mixed / jnp.maximum(total, 1.0).T[:, :, None])
        .astype(jnp.bfloat16)
        .reshape(tok_rows, local_width)
    )
    groups = tok_rows // 4
    rows = np.arange(tok_rows)
    quarter_order = jnp.asarray((rows % groups) * 4 + rows // groups, dtype=jnp.int32)

    def by_quarter(array):
        return jnp.take(array, quarter_order, axis=0, mode="clip")

    partial_attn = jnp.dot(by_quarter(attended), out_weight, preferred_element_type=jnp.float32)

    def pick_rows(array):
        return lax.dynamic_slice_in_dim(array, tensor_rank * groups, groups)

    valid_rows = pick_rows(by_quarter(valid_local)[:, None])
    attn_full = tensor_all_reduce(partial_attn.reshape(tensor_count, -1, width)).reshape(tok_rows, width)
    x0_rows = by_quarter(x0)
    x1 = x0_rows + attn_full.astype(jnp.float32)
    h2 = layer_norm(x1, ln2_gain).astype(jnp.bfloat16)
    hidden = jax.nn.gelu(
        jnp.dot(h2, fc1_weight, preferred_element_type=jnp.float32), approximate=False
    ).astype(jnp.bfloat16)
    mlp_out = jnp.dot(hidden, fc2_weight, preferred_element_type=jnp.float32)
    mlp_part = tensor_reduce_scatter(mlp_out.reshape(tensor_count, groups, width))
    x1_rows = pick_rows(x1)
    own_quarter = ((x1_rows + mlp_part) * valid_rows).astype(jnp.bfloat16)
    gathered = lax.all_to_all(
        jnp.broadcast_to(own_quarter, (seq_count,) + own_quarter.shape),
        "seq",
        split_axis=0,
        concat_axis=0,
        tiled=True,
    ).reshape(seq_count * groups, width)
    partial_proj = jnp.dot(gathered, proj_weight, preferred_element_type=jnp.float32)
    quarter_rows = seq_count * groups // tensor_count
    proj_part = tensor_reduce_scatter(partial_proj.reshape(tensor_count, quarter_rows, -1))
    row_begin = tensor_rank * quarter_rows
    merged_seg = lax.dynamic_slice_in_dim(seg_ids.reshape(-1, 4)[:, 0], row_begin, quarter_rows)
    merged_valid = lax.dynamic_slice_in_dim(pad_mask.reshape(-1, 4)[:, 0], row_begin, quarter_rows)
    image_ids = jnp.arange(image_sizes.shape[0], dtype=jnp.int32)
    member = ((merged_seg[:, None] == image_ids[None, :]) & (merged_valid[:, None] == 1)).astype(
        jnp.float32
    )
    row_squares = jnp.sum(proj_part * proj_part, axis=1)
    row_peak = jnp.max(jnp.abs(proj_part), axis=1)
    local_sums = jnp.dot(row_squares, member, precision=lax.Precision.HIGHEST)
    local_peaks = jnp.max(jnp.where(member > 0, row_peak[:, None], 0.0), axis=0)
    emb = proj_part.astype(jnp.bfloat16)
    capacity = 2 * quarter_rows // seq_count
    owner_rows = lax.dynamic_slice_in_dim(owners[:, 0], row_begin, quarter_rows)
    onehot = (owner_rows[:, None] == jnp.arange(seq_count, dtype=jnp.int32)[None, :]).astype(
        jnp.int32
    )
    rank = jnp.cumsum(onehot, axis=0) - onehot
    slot = jnp.sum(onehot * rank, axis=1)
    target = owner_rows * capacity + slot
    place = (jnp.arange(seq_count * capacity, dtype=jnp.int32)[:, None] == target[None, :]).astype(
        jnp.bfloat16
    )
    buffer = jnp.dot(place, emb, preferred_element_type=jnp.float32).astype(jnp.bfloat16)
    buffer = buffer.reshape(seq_count, capacity, emb.shape[1])
    stats = jnp.stack([local_sums, local_peaks]).reshape(-1)
    high = stats.astype(jnp.bfloat16)
    low = (stats - high.astype(jnp.float32)).astype(jnp.bfloat16)
    extra = jnp.zeros((8, emb.shape[1]), jnp.bfloat16)
    extra = extra.at[0, : stats.shape[0]].set(high).at[1, : stats.shape[0]].set(low)
    buffer = jnp.concatenate([buffer, jnp.broadcast_to(extra, (seq_count,) + extra.shape)], axis=1)
    arrived = lax.all_to_all(buffer, "seq", split_axis=0, concat_axis=2, tiled=True)
    delivered = arrived[:, :capacity].reshape(1, 1, capacity, arrived.shape[2])
    parts = arrived[0, capacity : capacity + 2].reshape(2, seq_count, emb.shape[1])
    parts = parts[:, :, : stats.shape[0]].astype(jnp.float32)
    parts = (parts[0] + parts[1]).reshape(seq_count, 2, -1)
    stats = jnp.stack([jnp.sum(parts[:, 0], axis=0), jnp.max(parts[:, 1], axis=0)])
    for bit in (1, 2):
        if bit < tensor_count:
            other = swap(stats, "tensor", bit)
            stats = jnp.stack([stats[0] + other[0], jnp.maximum(stats[1], other[1])])
    sums, image_peak = stats[0], stats[1]
    counts = (image_sizes[:, 0] * image_sizes[:, 1] // 4).astype(jnp.float32)
    image_rms = jnp.sqrt(sums / (PROJ * jnp.maximum(counts, 1.0)))
    return (delivered, image_rms, image_peak)


def solution(mesh):
    in_specs = (
        P(("dp", "seq"), None),
        P("dp", None),
        P("dp"),
        P("dp"),
        P(),
        P(None, None, "tensor"),
        P("tensor", None),
        P(),
        P(None, "tensor"),
        P("tensor", None),
        P("tensor", "seq"),
        P("dp", None),
    )
    out_specs = (P(("dp", "seq"), "tensor", None, None), P("dp"), P("dp"))

    return jax.shard_map(local, mesh=mesh, in_specs=in_specs, out_specs=out_specs, check_vma=False)
```

```python
import math

import jax
import numpy as np
import jax.numpy as jnp
from jax import lax
from jax.sharding import PartitionSpec as P

HD = 104
PROJ = 4096
SIDE = 32


EPS = 1e-06


def shifted(value, axis, steps):
    count = lax.axis_size(axis)
    leading, last = (max(0, -steps), min(count, count - steps))
    return lax.ppermute(value, axis, [(source, source + steps) for source in range(leading, last)])


def swap(value, axis, bit):
    count = lax.axis_size(axis)
    return lax.ppermute(value, axis, [(source, source ^ bit) for source in range(count)])


def take_half(value, index, axis):
    return lax.dynamic_index_in_dim(value, index, axis, keepdims=False)


def tensor_reduce_scatter(parts, rank=None):
    if rank is None:
        rank = lax.axis_index("tensor")
    low, high = rank % 2, rank // 2
    quads = parts.reshape((2, 2) + parts.shape[1:])
    kept = take_half(quads, low, 1)
    sent = take_half(quads, 1 - low, 1).astype(jnp.bfloat16)
    halves = kept + swap(sent, "tensor", 1).astype(jnp.float32)
    sent = take_half(halves, 1 - high, 0).astype(jnp.bfloat16)
    return take_half(halves, high, 0) + swap(sent, "tensor", 2).astype(jnp.float32)


def tensor_all_reduce(parts):
    rank = lax.axis_index("tensor")
    low = rank % 2
    quads = parts.reshape((2, 2) + parts.shape[1:])
    sent = take_half(quads, 1 - low, 1).astype(jnp.bfloat16)
    halves = (take_half(quads, low, 1) + swap(sent, "tensor", 1).astype(jnp.float32)).astype(jnp.bfloat16)
    total = (halves.astype(jnp.float32) + swap(halves, "tensor", 2).astype(jnp.float32)).astype(jnp.bfloat16)
    other = swap(total, "tensor", 1)
    return jnp.where(low == 0, jnp.stack([total, other], 1), jnp.stack([other, total], 1))


def layer_norm(values, gain):
    mean = jnp.mean(values, axis=-1, keepdims=True)
    centred = values - mean
    spread = jnp.mean(centred * centred, axis=-1, keepdims=True)
    return centred * lax.rsqrt(spread + EPS) * gain


def position_table(seg_local, image_sizes, index, width):
    heights = image_sizes[:, 0]
    widths = image_sizes[:, 1]
    areas = heights * widths
    starts = jnp.cumsum(areas) - areas
    image_ids = jnp.arange(image_sizes.shape[0], dtype=jnp.int32)
    member = (seg_local[:, None] == image_ids[None, :]).astype(jnp.int32)
    begin = jnp.sum(member * starts[None, :], axis=1)
    across = jnp.sum(member * widths[None, :], axis=1)
    offset = index - begin
    blocks = offset // 4
    inner = offset % 4
    half = jnp.maximum(across // 2, 1)
    row_pos = jnp.clip(2 * (blocks // half) + inner // 2, 0, SIDE - 1)
    col_pos = jnp.clip(2 * (blocks % half) + inner % 2, 0, SIDE - 1)
    quarter = width // 4
    freq = jnp.exp(jnp.arange(quarter, dtype=jnp.float32) * (-math.log(10000.0) / quarter))
    angle = jnp.arange(SIDE, dtype=jnp.float32)[:, None] * freq[None, :]
    table = jnp.concatenate([jnp.sin(angle), jnp.cos(angle)], axis=1)
    return jnp.concatenate(
        [jnp.take(table, row_pos, axis=0, mode="clip"), jnp.take(table, col_pos, axis=0, mode="clip")],
        axis=1,
    )


def key_labels(block_start, tok_rows, seg_ids, pad_mask):
    total = seg_ids.shape[0]
    index = block_start + jnp.arange(tok_rows, dtype=jnp.int32)
    inside = (index >= 0) & (index < total)
    clamped = jnp.clip(block_start, 0, total - tok_rows)
    seg_part = lax.dynamic_slice_in_dim(seg_ids, clamped, tok_rows)
    mask_part = lax.dynamic_slice_in_dim(pad_mask, clamped, tok_rows)
    return (jnp.where(inside, seg_part, -1), inside & (mask_part == 1))


def local(
    patches,
    image_sizes,
    seg_ids,
    pad_mask,
    ln1_gain,
    qkv_weight,
    out_weight,
    ln2_gain,
    fc1_weight,
    fc2_weight,
    proj_weight,
    owners,
):
    tok_rows, width = patches.shape
    seq_count = lax.axis_size("seq")
    tensor_count = lax.axis_size("tensor")
    seq_rank = lax.axis_index("seq")
    tensor_rank = lax.axis_index("tensor")
    first = seq_rank * tok_rows
    index = first + jnp.arange(tok_rows, dtype=jnp.int32)
    seg_local = lax.dynamic_slice_in_dim(seg_ids, first, tok_rows)
    valid_local = lax.dynamic_slice_in_dim(pad_mask, first, tok_rows).astype(jnp.float32)
    x0 = (
        patches.astype(jnp.float32)
        + position_table(seg_local, image_sizes, index, width) * valid_local[:, None]
    )
    h1 = layer_norm(x0, ln1_gain).astype(jnp.bfloat16)
    local_width = qkv_weight.shape[2]
    heads = local_width // HD
    pairs = jnp.einsum(
        "td,dkc->tkc", h1, qkv_weight[:, 1:], preferred_element_type=jnp.float32
    ).astype(jnp.bfloat16)
    queries = jnp.dot(h1, qkv_weight[:, 0], preferred_element_type=jnp.float32)
    queries = queries.astype(jnp.bfloat16).reshape(tok_rows, heads, HD)
    reach = min((SIDE * SIDE + tok_rows - 2) // tok_rows, seq_count - 1)
    blocks = [pairs]
    block_starts = [first]
    for step in range(1, reach + 1):
        blocks.append(shifted(pairs, "seq", step))
        block_starts.append(first - step * tok_rows)
        blocks.append(shifted(pairs, "seq", -step))
        block_starts.append(first + step * tok_rows)
    labels = [key_labels(start, tok_rows, seg_ids, pad_mask) for start in block_starts]
    key_seg = jnp.concatenate([item[0] for item in labels])
    key_ok = jnp.concatenate([item[1] for item in labels])
    gathered_pairs = jnp.concatenate(blocks, axis=0)
    keys = gathered_pairs[:, 0].reshape(-1, heads, HD)
    values = gathered_pairs[:, 1].reshape(-1, heads, HD)
    allowed = ((seg_local[:, None] == key_seg[None, :]) & key_ok[None, :])[None, :, :]
    scores = jnp.einsum("qhe,khe->hqk", queries, keys, preferred_element_type=jnp.float32) * HD ** (
        -0.5
    )
    best = jnp.max(jnp.where(allowed, scores, -1e30), axis=2, keepdims=True)
    weights = jnp.where(allowed, jnp.exp(scores - best), 0.0)
    total = jnp.sum(weights, axis=2)
    mixed = jnp.einsum(
        "hqk,khe->qhe", weights.astype(jnp.bfloat16), values, preferred_element_type=jnp.float32
    )
    attended = (
        (mixed / jnp.maximum(total, 1.0).T[:, :, None])
        .astype(jnp.bfloat16)
        .reshape(tok_rows, local_width)
    )
    groups = tok_rows // 4
    rows = np.arange(tok_rows)
    quarter_order = jnp.asarray((rows % groups) * 4 + rows // groups, dtype=jnp.int32)

    def by_quarter(array):
        return jnp.take(array, quarter_order, axis=0, mode="clip")

    partial_attn = jnp.dot(by_quarter(attended), out_weight, preferred_element_type=jnp.float32)

    def pick_rows(array):
        return lax.dynamic_slice_in_dim(array, tensor_rank * groups, groups)

    valid_rows = pick_rows(by_quarter(valid_local)[:, None])
    attn_full = tensor_all_reduce(partial_attn.reshape(tensor_count, -1, width)).reshape(tok_rows, width)
    x0_rows = by_quarter(x0)
    x1 = x0_rows + attn_full.astype(jnp.float32)
    h2 = layer_norm(x1, ln2_gain).astype(jnp.bfloat16)
    hidden = jax.nn.gelu(
        jnp.dot(h2, fc1_weight, preferred_element_type=jnp.float32), approximate=False
    ).astype(jnp.bfloat16)
    mlp_out = jnp.dot(hidden, fc2_weight, preferred_element_type=jnp.float32)
    mlp_part = tensor_reduce_scatter(mlp_out.reshape(tensor_count, groups, width))
    x1_rows = pick_rows(x1)
    own_quarter = ((x1_rows + mlp_part) * valid_rows).astype(jnp.bfloat16)
    gathered = lax.all_to_all(
        jnp.broadcast_to(own_quarter, (seq_count,) + own_quarter.shape),
        "seq",
        split_axis=0,
        concat_axis=0,
        tiled=True,
    ).reshape(seq_count * groups, width)
    partial_proj = jnp.dot(gathered, proj_weight, preferred_element_type=jnp.float32)
    quarter_rows = seq_count * groups // tensor_count
    proj_part = tensor_reduce_scatter(partial_proj.reshape(tensor_count, quarter_rows, -1))
    row_begin = tensor_rank * quarter_rows
    merged_seg = lax.dynamic_slice_in_dim(seg_ids.reshape(-1, 4)[:, 0], row_begin, quarter_rows)
    merged_valid = lax.dynamic_slice_in_dim(pad_mask.reshape(-1, 4)[:, 0], row_begin, quarter_rows)
    image_ids = jnp.arange(image_sizes.shape[0], dtype=jnp.int32)
    member = ((merged_seg[:, None] == image_ids[None, :]) & (merged_valid[:, None] == 1)).astype(
        jnp.float32
    )
    row_squares = jnp.sum(proj_part * proj_part, axis=1)
    row_peak = jnp.max(jnp.abs(proj_part), axis=1)
    local_sums = jnp.dot(row_squares, member, precision=lax.Precision.HIGHEST)
    local_peaks = jnp.max(jnp.where(member > 0, row_peak[:, None], 0.0), axis=0)
    emb = proj_part.astype(jnp.bfloat16)
    capacity = 2 * quarter_rows // seq_count
    owner_rows = lax.dynamic_slice_in_dim(owners[:, 0], row_begin, quarter_rows)
    onehot = (owner_rows[:, None] == jnp.arange(seq_count, dtype=jnp.int32)[None, :]).astype(
        jnp.int32
    )
    rank = jnp.cumsum(onehot, axis=0) - onehot
    slot = jnp.sum(onehot * rank, axis=1)
    target = owner_rows * capacity + slot
    place = (jnp.arange(seq_count * capacity, dtype=jnp.int32)[:, None] == target[None, :]).astype(
        jnp.bfloat16
    )
    buffer = jnp.dot(place, emb, preferred_element_type=jnp.float32).astype(jnp.bfloat16)
    buffer = buffer.reshape(seq_count, capacity, emb.shape[1])
    stats = jnp.stack([local_sums, local_peaks]).reshape(-1)
    high = stats.astype(jnp.bfloat16)
    low = (stats - high.astype(jnp.float32)).astype(jnp.bfloat16)
    extra = jnp.zeros((8, emb.shape[1]), jnp.bfloat16)
    extra = extra.at[0, : stats.shape[0]].set(high).at[1, : stats.shape[0]].set(low)
    buffer = jnp.concatenate([buffer, jnp.broadcast_to(extra, (seq_count,) + extra.shape)], axis=1)
    arrived = lax.all_to_all(buffer, "seq", split_axis=0, concat_axis=2, tiled=True)
    delivered = arrived[:, :capacity].reshape(1, 1, capacity, arrived.shape[2])
    parts = arrived[0, capacity : capacity + 2].reshape(2, seq_count, emb.shape[1])
    parts = parts[:, :, : stats.shape[0]].astype(jnp.float32)
    parts = (parts[0] + parts[1]).reshape(seq_count, 2, -1)
    stats = jnp.stack([jnp.sum(parts[:, 0], axis=0), jnp.max(parts[:, 1], axis=0)])
    for bit in (1, 2):
        if bit < tensor_count:
            other = swap(stats, "tensor", bit)
            stats = jnp.stack([stats[0] + other[0], jnp.maximum(stats[1], other[1])])
    sums, image_peak = stats[0], stats[1]
    counts = (image_sizes[:, 0] * image_sizes[:, 1] // 4).astype(jnp.float32)
    image_rms = jnp.sqrt(sums / (PROJ * jnp.maximum(counts, 1.0)))
    return (delivered, image_rms, image_peak)


def solution(mesh):
    in_specs = (
        P(("dp", "seq"), None),
        P("dp", None),
        P("dp"),
        P("dp"),
        P(),
        P(None, None, "tensor"),
        P("tensor", None),
        P(),
        P(None, "tensor"),
        P("tensor", None),
        P("tensor", "seq"),
        P("dp", None),
    )
    out_specs = (P(("dp", "seq"), "tensor", None, None), P("dp"), P("dp"))

    return jax.shard_map(local, mesh=mesh, in_specs=in_specs, out_specs=out_specs, check_vma=False)
```
